512 devices in a mesh: rows: 64 (over y, z), cols: 8 (over x, core).
Axes of the slice: x: 4, y: 8, z: 8, core: 2. Of those that a mesh axis runs over, the one named last changes fastest.
Arguments:
- queries: bfloat16 [32768, 128], P('rows'), may hold values from -1 to 1
- prototypes: bfloat16 [16384, 128], P('cols'), may hold values from -1 to 1
- potential: float32 [16384], P('cols'), may hold values from -0.15 to 0.15
- weights: int32 [32768], P('rows'), may hold values from 1 to 10, as said below
- capacity: int32 [16384], P('cols'), may hold values from 1 to 7, as said below
- cotangent: bfloat16 [32768, 128], P('rows'), may hold values from -16 to 16
Outputs:
- grad_queries: float32 [32768, 128], P(('rows', 'cols'))
- grad_protos: float32 [16384, 128], P('cols')
The draws below stay inside these ranges and needn't reach their ends.
Inputs may be any that keep to these rules, and one draw needn't show every extreme that they name: weights rise along the queries: the first quarter are all 1, the k-th quarter (k = 0..3) lies in 1 + k to 1 + 3 k. `capacity`: capacities rise along the slots: the k-th quarter (k = 0..3) lies in 1 + k to 1 + 2 k.
All inputs are finite; a program needn't handle non-finite values.
Results may differ from the reference program's by a relative error of at most 0.0019.
The reference program's roundings to bfloat16 on the way (of `qhat`, `phat` and `scaled`) count: a program that leaves them out, or rounds other values in their place, can miss the bound.
Values sent between devices are 32-bit elements; how exact they have to be, the bound alone decides.
No kernel may reach another device: no remote copies, remote signals or barrier semaphores. Data moves between devices by JAX's collectives and lax.ppermute only.
A program may use at most 64 MiB of HBM per device.

```python
import math
import jax
import jax.numpy as jnp
from jax import lax

F = 128
NS = 16384
NQ = 32768


def draw_weights(key, part):
    index = jnp.arange(NQ, dtype=jnp.int32)
    level = 4 * index // NQ
    return jax.random.randint(jax.random.fold_in(key, 11), (NQ,), 1 + level, 2 + 3 * level, dtype=jnp.int32)


def draw_capacity(key, part):
    index = jnp.arange(NS, dtype=jnp.int32)
    level = 4 * index // NS
    return jax.random.randint(jax.random.fold_in(key, 23), (NS,), 1 + level, 2 + 2 * level, dtype=jnp.int32)


def harmonic_rows(bearing, radius, jitter):
    columns = [radius * jnp.cos(bearing), radius * jnp.sin(bearing)]
    for harmonic in range(2, 6):
        columns.append(0.15 * jnp.cos(harmonic * bearing))
        columns.append(0.15 * jnp.sin(harmonic * bearing))
    signal = jnp.stack(columns, axis=1)
    signal = jnp.pad(signal, ((0, 0), (0, jitter.shape[1] - 10)))
    return jnp.clip(signal + jitter, -1.0, 1.0)


def draw_queries(key, part):
    subkeys = jax.random.split(jax.random.fold_in(key, 41), 3)
    bearing = jax.random.uniform(subkeys[0], (NQ,), jnp.float32, -jnp.pi, jnp.pi)
    radius = jax.random.uniform(subkeys[1], (NQ,), jnp.float32, 0.55, 1.1)
    jitter = jax.random.normal(subkeys[2], (NQ, F), jnp.float32) * (0.5 / F) ** 0.5
    return harmonic_rows(bearing, radius, jitter).astype(jnp.bfloat16)


def draw_prototypes(key, part):
    subkeys = jax.random.split(jax.random.fold_in(key, 43), 3)
    bearing = jax.random.uniform(subkeys[0], (NS,), jnp.float32, -jnp.pi, jnp.pi)
    radius = jax.random.uniform(subkeys[1], (NS,), jnp.float32, 0.55, 1.1)
    jitter = jax.random.normal(subkeys[2], (NS, F), jnp.float32) * (0.5 / F) ** 0.5
    return harmonic_rows(bearing, radius, jitter).astype(jnp.bfloat16)


def draw_cotangent(key, part):
    subkeys = jax.random.split(jax.random.fold_in(key, 47), 2)
    polarity = 2.0 * jax.random.randint(subkeys[0], (8,), 0, 2).astype(jnp.float32) - 1.0
    strength = 3.0
    jitter = jax.random.normal(subkeys[1], (NQ, F), jnp.float32) * 4.0
    offset = jnp.concatenate([jnp.zeros((2,), jnp.float32), strength * polarity, jnp.zeros((F - 10,), jnp.float32)])
    return jnp.clip(jitter + offset[None, :], -16.0, 16.0).astype(jnp.bfloat16)


def level_of(stream_key, extent, cuts, least, high):
    level = 1.0
    for axis_at, parts in cuts:
        heights = jax.random.uniform(jax.random.fold_in(jax.random.fold_in(stream_key, 6), axis_at), (parts,), jnp.float32, least / len(cuts), high / len(cuts))
        level = level * jnp.repeat(jnp.exp(heights), extent[axis_at] // parts).reshape((-1,) + (1,) * (len(extent) - 1 - axis_at))
    return level


def setup_inputs(seed: int = 0) -> dict:
    streams_of = jax.random.split(jax.random.key(seed), 7)
    return {
        "queries": draw_queries(jax.random.fold_in(streams_of[6], 71), 0),
        "prototypes": draw_prototypes(jax.random.fold_in(streams_of[6], 71), 0),
        "potential": jnp.clip(jax.random.uniform(streams_of[2], (NS,), jnp.float32, -0.15, 0.15) * level_of(streams_of[2], (NS,), ((0, 8),), -0.4, 0.0), -0.15, 0.15),
        "weights": draw_weights(jax.random.fold_in(streams_of[6], 71), 0),
        "capacity": draw_capacity(jax.random.fold_in(streams_of[6], 71), 0),
        "cotangent": draw_cotangent(jax.random.fold_in(streams_of[6], 71), 0),
    }


TEMPER = 0.05

def unit_rows(matrix):
    wide = matrix.astype(jnp.float32)
    length = jnp.sqrt(lax.optimization_barrier(jnp.sum(wide * wide, axis=1)) + 1e-06)
    return ((wide / length[:, None]).astype(jnp.bfloat16), length)

def unit_back(grad, unit, length):
    wide = unit.astype(jnp.float32)
    along = lax.optimization_barrier(jnp.sum(wide * grad, axis=1, keepdims=True))
    return (grad - wide * along) / length[:, None]

def pair_dot(left, right):
    return lax.dot_general(left, right, (((1,), (1,)), ((), ())), preferred_element_type=jnp.float32)

def kernel_tile(qrows, phat, potential, capacity):
    scores = pair_dot(qrows, phat)
    return capacity.astype(jnp.float32)[None, :] * jnp.exp((scores - potential[None, :]) / TEMPER)

def reference(queries, prototypes, potential, weights, capacity, cotangent):
    qhat, qlen = unit_rows(queries)
    phat, plen = unit_rows(prototypes)
    wgt = weights.astype(jnp.float32)
    scaled = (cotangent.astype(jnp.float32) / wgt[:, None]).astype(jnp.bfloat16)
    total = qhat.shape[0]
    feats = qhat.shape[1]
    slots = phat.shape[0]
    block = math.gcd(total, 256)
    count = total // block
    qblocks = qhat.reshape(count, block, feats)
    sblocks = scaled.reshape(count, block, feats)
    wblocks = wgt.reshape(count, block)

    def first(args):
        qrows, srows = args
        kern = kernel_tile(qrows, phat, potential, capacity)
        coupling = pair_dot(srows, phat)
        return (lax.optimization_barrier(jnp.sum(kern, axis=1)), lax.optimization_barrier(jnp.sum(kern * coupling, axis=1)))
    ztot, kgsum = lax.map(first, (qblocks, sblocks))
    share = wblocks / ztot
    pvec = share * kgsum
    alpha_one = pvec / wblocks

    def second(carry, args):
        qrows, srows, srate, arow = args
        kern = kernel_tile(qrows, phat, potential, capacity)
        coupling = pair_dot(srows, phat)
        plan = srate[:, None] * kern
        return ((carry[0] + lax.optimization_barrier(jnp.sum(plan, axis=0)), carry[1] + lax.optimization_barrier(jnp.sum(plan * coupling, axis=0)), carry[2] + lax.optimization_barrier(jnp.sum(arow[:, None] * plan, axis=0))), None)
    empty = jnp.zeros((slots,), jnp.float32)
    (colsum, qvec, t_one), _ = lax.scan(second, (empty, empty, empty), (qblocks, sblocks, share, alpha_one))
    beta_one = (qvec - t_one) / colsum

    def third(args):
        qrows, srate = args
        plan = srate[:, None] * kernel_tile(qrows, phat, potential, capacity)
        return lax.optimization_barrier(jnp.sum(plan * beta_one[None, :], axis=1))
    rowprod = lax.map(third, (qblocks, share))
    alpha_two = (pvec - rowprod) / wblocks

    def fourth(carry, args):
        qrows, srate, arow = args
        plan = srate[:, None] * kernel_tile(qrows, phat, potential, capacity)
        return (carry + lax.optimization_barrier(jnp.sum(arow[:, None] * plan, axis=0)), None)
    t_two, _ = lax.scan(fourth, empty, (qblocks, share, alpha_two))
    beta_two = (qvec - t_two) / colsum

    def fifth(carry, args):
        qrows, srows, srate, arow = args
        kern = kernel_tile(qrows, phat, potential, capacity)
        coupling = pair_dot(srows, phat)
        plan = srate[:, None] * kern
        dscore = (plan * (coupling - arow[:, None] - beta_two[None, :]) / TEMPER).astype(jnp.bfloat16)
        planb = plan.astype(jnp.bfloat16)
        dq = jnp.dot(dscore, phat, preferred_element_type=jnp.float32)
        dp = lax.dot_general(dscore, qrows, (((0,), (0,)), ((), ())), preferred_element_type=jnp.float32)
        dp = dp + lax.dot_general(planb, srows, (((0,), (0,)), ((), ())), preferred_element_type=jnp.float32)
        return (carry + dp, dq)
    dphat, dqhat = lax.scan(fifth, jnp.zeros((slots, feats), jnp.float32), (qblocks, sblocks, share, alpha_two))
    grad_queries = unit_back(dqhat.reshape(total, feats), qhat, qlen)
    grad_protos = unit_back(dphat, phat, plen)
    return (grad_queries, grad_protos)
```

```python
import functools
import math

import jax
import jax.numpy as jnp
from jax import lax
from jax.sharding import PartitionSpec as P

TEMPER = 0.05


def unit_rows(matrix):
    wide = matrix.astype(jnp.float32)
    length = jnp.sqrt(jnp.sum(wide * wide, axis=1) + 1e-06)
    return ((wide / length[:, None]).astype(jnp.bfloat16), length)


def unit_back(grad, unit, length):
    wide = unit.astype(jnp.float32)
    along = jnp.sum(wide * grad, axis=1, keepdims=True)
    return (grad - wide * along) / length[:, None]


def pair_dot(left, right):
    return lax.dot_general(
        left, right, (((1,), (1,)), ((), ())), preferred_element_type=jnp.float32
    )


def across_slots(stack):
    return lax.psum(stack, "cols")


def across_queries(stack, count):
    if count & (count - 1):
        return lax.psum(stack, "rows")
    step = 1
    while step < count:
        pairs = [(i, i ^ step) for i in range(count)]
        stack = stack + lax.ppermute(stack, "rows", pairs)
        step *= 2
    return stack


def local(count, queries, prototypes, potential, weights, capacity, cotangent):
    qhat, qlen = unit_rows(queries)
    phat, plen = unit_rows(prototypes)
    wgt = weights.astype(jnp.float32)
    scaled = (cotangent.astype(jnp.float32) / wgt[:, None]).astype(jnp.bfloat16)
    local_rows = qhat.shape[0]
    slots = phat.shape[0]
    width = math.gcd(slots, 512)
    starts = list(range(0, slots, width))

    def kernel_tile(start):
        scores = pair_dot(qhat, phat[start : start + width])
        weight_cols = capacity[start : start + width].astype(jnp.float32)
        return weight_cols[None, :] * jnp.exp(
            (scores - potential[start : start + width][None, :]) / TEMPER
        )

    def coupling_tile(start):
        return pair_dot(scaled, phat[start : start + width])

    ztot = jnp.zeros((local_rows,), jnp.float32)
    kgsum = jnp.zeros((local_rows,), jnp.float32)
    for start in starts:
        kern = kernel_tile(start)
        ztot = ztot + jnp.sum(kern, axis=1)
        kgsum = kgsum + jnp.sum(kern * coupling_tile(start), axis=1)
    totals = across_slots(jnp.stack([ztot, kgsum]))
    share = wgt / totals[0]
    pvec = share * totals[1]
    alpha_one = pvec / wgt
    col_parts, q_parts, t_parts = ([], [], [])
    for start in starts:
        plan = share[:, None] * kernel_tile(start)
        col_parts.append(jnp.sum(plan, axis=0))
        q_parts.append(jnp.sum(plan * coupling_tile(start), axis=0))
    for start in starts:
        plan = share[:, None] * kernel_tile(start)
        t_parts.append(jnp.sum(alpha_one[:, None] * plan, axis=0))
    summed = across_queries(
        jnp.stack([jnp.concatenate(col_parts), jnp.concatenate(q_parts), jnp.concatenate(t_parts)]),
        count,
    )
    colsum, qvec, t_one = (summed[0], summed[1], summed[2])
    beta_one = (qvec - t_one) / colsum
    rowprod = jnp.zeros((local_rows,), jnp.float32)
    for start in starts:
        plan = share[:, None] * kernel_tile(start)
        rowprod = rowprod + jnp.sum(plan * beta_one[start : start + width][None, :], axis=1)
    rowprod = across_slots(rowprod[None, :])[0]
    alpha_two = (pvec - rowprod) / wgt
    t_parts = []
    for start in starts:
        plan = share[:, None] * kernel_tile(start)
        t_parts.append(jnp.sum(alpha_two[:, None] * plan, axis=0))
    t_two = across_queries(jnp.concatenate(t_parts)[None, :], count)[0]
    beta_two = (qvec - t_two) / colsum
    dqhat = jnp.zeros(qhat.shape, jnp.float32)
    dp_parts = []
    for start in starts:
        plan = share[:, None] * kernel_tile(start)
        coupling = coupling_tile(start)
        shift_cols = beta_two[start : start + width][None, :]
        dscore = (plan * (coupling - alpha_two[:, None] - shift_cols) / TEMPER).astype(jnp.bfloat16)
        planb = plan.astype(jnp.bfloat16)
        dqhat = dqhat + jnp.dot(
            dscore, phat[start : start + width], preferred_element_type=jnp.float32
        )
        part = lax.dot_general(
            dscore, qhat, (((0,), (0,)), ((), ())), preferred_element_type=jnp.float32
        )
        part = part + lax.dot_general(
            planb, scaled, (((0,), (0,)), ((), ())), preferred_element_type=jnp.float32
        )
        dp_parts.append(part)
    dphat = jnp.concatenate(dp_parts, axis=0)
    query_part = lax.psum_scatter(dqhat, "cols", scatter_dimension=0, tiled=True)
    piece = query_part.shape[0]
    begin = lax.axis_index("cols") * piece
    grad_queries = unit_back(
        query_part,
        lax.dynamic_slice_in_dim(qhat, begin, piece, 0),
        lax.dynamic_slice_in_dim(qlen, begin, piece, 0),
    )
    whole = lax.psum(dphat, "rows")
    grad_protos = unit_back(whole, phat, plen)
    return (grad_queries, grad_protos)


def solution(mesh):
    in_specs = (P("rows", None), P("cols", None), P("cols"), P("rows"), P("cols"), P("rows", None))
    out_specs = (P(("rows", "cols"), None), P("cols", None))
    body = functools.partial(local, mesh.shape["rows"])
    return jax.shard_map(body, mesh=mesh, in_specs=in_specs, out_specs=out_specs, check_vma=False)
```

```python
import functools
import math

import jax
import jax.numpy as jnp
from jax import lax
from jax.sharding import PartitionSpec as P

TEMPER = 0.05


def unit_rows(matrix):
    wide = matrix.astype(jnp.float32)
    length = jnp.sqrt(jnp.sum(wide * wide, axis=1) + 1e-06)
    return ((wide / length[:, None]).astype(jnp.bfloat16), length)


def unit_back(grad, unit, length):
    wide = unit.astype(jnp.float32)
    along = jnp.sum(wide * grad, axis=1, keepdims=True)
    return (grad - wide * along) / length[:, None]


def pair_dot(left, right):
    return lax.dot_general(
        left, right, (((1,), (1,)), ((), ())), preferred_element_type=jnp.float32
    )


def across_slots(stack):
    return lax.psum(stack, "cols")


def across_queries(stack, count):
    if count & (count - 1):
        return lax.psum(stack, "rows")
    step = 1
    while step < count:
        pairs = [(i, i ^ step) for i in range(count)]
        stack = stack + lax.ppermute(stack, "rows", pairs)
        step *= 2
    return stack


def halving_scatter(block, axis, count):
    where = lax.axis_index(axis)
    step = count // 2
    while step >= 1:
        half = block.shape[0] // 2
        bit = (where // step) % 2
        keep = lax.dynamic_slice_in_dim(block, bit * half, half, 0)
        send = lax.dynamic_slice_in_dim(block, (1 - bit) * half, half, 0)
        pairs = [(i, i ^ step) for i in range(count)]
        block = keep + lax.ppermute(send, axis, pairs)
        step //= 2
    return block


def local(count, width_cols, queries, prototypes, potential, weights, capacity, cotangent):
    qhat, qlen = unit_rows(queries)
    phat, plen = unit_rows(prototypes)
    wgt = weights.astype(jnp.float32)
    scaled = (cotangent.astype(jnp.float32) / wgt[:, None]).astype(jnp.bfloat16)
    local_rows = qhat.shape[0]
    slots = phat.shape[0]
    width = math.gcd(slots, 512)
    starts = list(range(0, slots, width))

    def kernel_tile(start):
        scores = pair_dot(qhat, phat[start : start + width])
        weight_cols = capacity[start : start + width].astype(jnp.float32)
        return weight_cols[None, :] * jnp.exp(
            (scores - potential[start : start + width][None, :]) / TEMPER
        )

    def coupling_tile(start):
        return pair_dot(scaled, phat[start : start + width])

    ztot = jnp.zeros((local_rows,), jnp.float32)
    kgsum = jnp.zeros((local_rows,), jnp.float32)
    for start in starts:
        kern = kernel_tile(start)
        ztot = ztot + jnp.sum(kern, axis=1)
        kgsum = kgsum + jnp.sum(kern * coupling_tile(start), axis=1)
    totals = across_slots(jnp.stack([ztot, kgsum]))
    share = wgt / totals[0]
    pvec = share * totals[1]
    alpha_one = pvec / wgt
    col_parts, q_parts, t_parts = ([], [], [])
    for start in starts:
        plan = share[:, None] * kernel_tile(start)
        col_parts.append(jnp.sum(plan, axis=0))
        q_parts.append(jnp.sum(plan * coupling_tile(start), axis=0))
    for start in starts:
        plan = share[:, None] * kernel_tile(start)
        t_parts.append(jnp.sum(alpha_one[:, None] * plan, axis=0))
    summed = across_queries(
        jnp.stack([jnp.concatenate(col_parts), jnp.concatenate(q_parts), jnp.concatenate(t_parts)]),
        count,
    )
    colsum, qvec, t_one = (summed[0], summed[1], summed[2])
    beta_one = (qvec - t_one) / colsum
    rowprod = jnp.zeros((local_rows,), jnp.float32)
    for start in starts:
        plan = share[:, None] * kernel_tile(start)
        rowprod = rowprod + jnp.sum(plan * beta_one[start : start + width][None, :], axis=1)
    rowprod = across_slots(rowprod[None, :])[0]
    alpha_two = (pvec - rowprod) / wgt
    t_parts = []
    for start in starts:
        plan = share[:, None] * kernel_tile(start)
        t_parts.append(jnp.sum(alpha_two[:, None] * plan, axis=0))
    t_two = across_queries(jnp.concatenate(t_parts)[None, :], count)[0]
    beta_two = (qvec - t_two) / colsum
    dqhat = jnp.zeros(qhat.shape, jnp.float32)
    dp_parts = []
    for start in starts:
        plan = share[:, None] * kernel_tile(start)
        coupling = coupling_tile(start)
        shift_cols = beta_two[start : start + width][None, :]
        dscore = (plan * (coupling - alpha_two[:, None] - shift_cols) / TEMPER).astype(jnp.bfloat16)
        planb = plan.astype(jnp.bfloat16)
        dqhat = dqhat + jnp.dot(
            dscore, phat[start : start + width], preferred_element_type=jnp.float32
        )
        part = lax.dot_general(
            dscore, qhat, (((0,), (0,)), ((), ())), preferred_element_type=jnp.float32
        )
        part = part + lax.dot_general(
            planb, scaled, (((0,), (0,)), ((), ())), preferred_element_type=jnp.float32
        )
        dp_parts.append(part)
    dphat = jnp.concatenate(dp_parts, axis=0)
    if width_cols & (width_cols - 1) or local_rows % width_cols:
        query_part = lax.psum_scatter(dqhat, "cols", scatter_dimension=0, tiled=True)
    else:
        query_part = halving_scatter(dqhat, "cols", width_cols)
    piece = query_part.shape[0]
    begin = lax.axis_index("cols") * piece
    grad_queries = unit_back(
        query_part,
        lax.dynamic_slice_in_dim(qhat, begin, piece, 0),
        lax.dynamic_slice_in_dim(qlen, begin, piece, 0),
    )
    whole = lax.psum(dphat, "rows")
    grad_protos = unit_back(whole, phat, plen)
    return (grad_queries, grad_protos)


def solution(mesh):
    in_specs = (P("rows", None), P("cols", None), P("cols"), P("rows"), P("cols"), P("rows", None))
    out_specs = (P(("rows", "cols"), None), P("cols", None))
    body = functools.partial(local, mesh.shape["rows"], mesh.shape["cols"])
    return jax.shard_map(body, mesh=mesh, in_specs=in_specs, out_specs=out_specs, check_vma=False)
```

```python
import functools
import itertools
import math

import jax
import jax.numpy as jnp
from jax import lax
from jax.sharding import PartitionSpec as P

TEMPER = 0.05


def unit_rows(matrix):
    wide = matrix.astype(jnp.float32)
    length = jnp.sqrt(jnp.sum(wide * wide, axis=1) + 1e-06)
    return ((wide / length[:, None]).astype(jnp.bfloat16), length)


def unit_back(grad, unit, length):
    wide = unit.astype(jnp.float32)
    along = jnp.sum(wide * grad, axis=1, keepdims=True)
    return (grad - wide * along) / length[:, None]


def pair_dot(left, right):
    return lax.dot_general(
        left, right, (((1,), (1,)), ((), ())), preferred_element_type=jnp.float32
    )


def across_slots(stack):
    return lax.psum(stack, "cols")


def across_queries(stack, count):
    if count & (count - 1):
        return lax.psum(stack, "rows")
    step = 1
    while step < count:
        pairs = [(i, i ^ step) for i in range(count)]
        stack = stack + lax.ppermute(stack, "rows", pairs)
        step *= 2
    return stack


def halving_scatter(block, axis, count):
    where = lax.axis_index(axis)
    step = count // 2
    while step >= 1:
        half = block.shape[0] // 2
        bit = (where // step) % 2
        keep = lax.dynamic_slice_in_dim(block, bit * half, half, 0)
        send = lax.dynamic_slice_in_dim(block, (1 - bit) * half, half, 0)
        pairs = [(i, i ^ step) for i in range(count)]
        block = keep + lax.ppermute(send, axis, pairs)
        step //= 2
    return block


def butterfly(block, axis, count, order):
    where = lax.axis_index(axis)
    for step in order:
        half = block.shape[0] // 2
        bit = (where // step) % 2
        keep = lax.dynamic_slice_in_dim(block, bit * half, half, 0)
        send = lax.dynamic_slice_in_dim(block, (1 - bit) * half, half, 0)
        pairs = [(i, i ^ step) for i in range(count)]
        block = keep + lax.ppermute(send, axis, pairs)
    for step in reversed(order):
        bit = (where // step) % 2
        pairs = [(i, i ^ step) for i in range(count)]
        other = lax.ppermute(block, axis, pairs)
        block = jnp.where(bit == 0, jnp.concatenate([block, other]), jnp.concatenate([other, block]))
    return block


def whole_sum(block, count, inner):
    bits = [1 << k for k in range(count.bit_length() - 1)]
    if count & (count - 1) or inner >= count or block.shape[0] % (2 * count):
        return lax.psum(block, "rows")
    low = [b for b in bits if b < inner]
    high = [b for b in bits if b >= inner]
    half = block.shape[0] // 2
    first = butterfly(block[:half], "rows", count, low + high)
    second = butterfly(block[half:], "rows", count, high + low)
    return jnp.concatenate([first, second])


def local(count, inner, width_cols, queries, prototypes, potential, weights, capacity, cotangent):
    qhat, qlen = unit_rows(queries)
    phat, plen = unit_rows(prototypes)
    wgt = weights.astype(jnp.float32)
    scaled = (cotangent.astype(jnp.float32) / wgt[:, None]).astype(jnp.bfloat16)
    local_rows = qhat.shape[0]
    slots = phat.shape[0]
    width = math.gcd(slots, 512)
    starts = list(range(0, slots, width))

    def kernel_tile(start):
        scores = pair_dot(qhat, phat[start : start + width])
        weight_cols = capacity[start : start + width].astype(jnp.float32)
        return weight_cols[None, :] * jnp.exp(
            (scores - potential[start : start + width][None, :]) / TEMPER
        )

    def coupling_tile(start):
        return pair_dot(scaled, phat[start : start + width])

    ztot = jnp.zeros((local_rows,), jnp.float32)
    kgsum = jnp.zeros((local_rows,), jnp.float32)
    for start in starts:
        kern = kernel_tile(start)
        ztot = ztot + jnp.sum(kern, axis=1)
        kgsum = kgsum + jnp.sum(kern * coupling_tile(start), axis=1)
    totals = across_slots(jnp.stack([ztot, kgsum]))
    share = wgt / totals[0]
    pvec = share * totals[1]
    alpha_one = pvec / wgt
    col_parts, q_parts, t_parts = ([], [], [])
    for start in starts:
        plan = share[:, None] * kernel_tile(start)
        col_parts.append(jnp.sum(plan, axis=0))
        q_parts.append(jnp.sum(plan * coupling_tile(start), axis=0))
    for start in starts:
        plan = share[:, None] * kernel_tile(start)
        t_parts.append(jnp.sum(alpha_one[:, None] * plan, axis=0))
    summed = across_queries(
        jnp.stack([jnp.concatenate(col_parts), jnp.concatenate(q_parts), jnp.concatenate(t_parts)]),
        count,
    )
    colsum, qvec, t_one = (summed[0], summed[1], summed[2])
    beta_one = (qvec - t_one) / colsum
    rowprod = jnp.zeros((local_rows,), jnp.float32)
    for start in starts:
        plan = share[:, None] * kernel_tile(start)
        rowprod = rowprod + jnp.sum(plan * beta_one[start : start + width][None, :], axis=1)
    rowprod = across_slots(rowprod[None, :])[0]
    alpha_two = (pvec - rowprod) / wgt
    t_parts = []
    for start in starts:
        plan = share[:, None] * kernel_tile(start)
        t_parts.append(jnp.sum(alpha_two[:, None] * plan, axis=0))
    t_two = across_queries(jnp.concatenate(t_parts)[None, :], count)[0]
    beta_two = (qvec - t_two) / colsum
    dqhat = jnp.zeros(qhat.shape, jnp.float32)
    dp_parts = []
    for start in starts:
        plan = share[:, None] * kernel_tile(start)
        coupling = coupling_tile(start)
        shift_cols = beta_two[start : start + width][None, :]
        dscore = (plan * (coupling - alpha_two[:, None] - shift_cols) / TEMPER).astype(jnp.bfloat16)
        planb = plan.astype(jnp.bfloat16)
        dqhat = dqhat + jnp.dot(
            dscore, phat[start : start + width], preferred_element_type=jnp.float32
        )
        part = lax.dot_general(
            dscore, qhat, (((0,), (0,)), ((), ())), preferred_element_type=jnp.float32
        )
        part = part + lax.dot_general(
            planb, scaled, (((0,), (0,)), ((), ())), preferred_element_type=jnp.float32
        )
        dp_parts.append(part)
    dphat = jnp.concatenate(dp_parts, axis=0)
    if width_cols & (width_cols - 1) or local_rows % width_cols:
        query_part = lax.psum_scatter(dqhat, "cols", scatter_dimension=0, tiled=True)
    else:
        query_part = halving_scatter(dqhat, "cols", width_cols)
    piece = query_part.shape[0]
    begin = lax.axis_index("cols") * piece
    grad_queries = unit_back(
        query_part,
        lax.dynamic_slice_in_dim(qhat, begin, piece, 0),
        lax.dynamic_slice_in_dim(qlen, begin, piece, 0),
    )
    whole = whole_sum(dphat, count, inner)
    grad_protos = unit_back(whole, phat, plen)
    return (grad_queries, grad_protos)


def inner_of(mesh):
    column = list(mesh.devices[:, 0])
    try:
        lead = column[0].coords[1]
        return sum(1 for _ in itertools.takewhile(lambda d: d.coords[1] == lead, column))
    except (AttributeError, IndexError):
        return len(column)


def solution(mesh):
    in_specs = (P("rows", None), P("cols", None), P("cols"), P("rows"), P("cols"), P("rows", None))
    out_specs = (P(("rows", "cols"), None), P("cols", None))
    body = functools.partial(local, mesh.shape["rows"], inner_of(mesh), mesh.shape["cols"])
    return jax.shard_map(body, mesh=mesh, in_specs=in_specs, out_specs=out_specs, check_vma=False)
```

```python
import functools
import itertools
import math

import jax
import jax.numpy as jnp
from jax import lax
from jax.sharding import PartitionSpec as P

TEMPER = 0.05


def unit_rows(matrix):
    wide = matrix.astype(jnp.float32)
    length = jnp.sqrt(jnp.sum(wide * wide, axis=1) + 1e-06)
    return ((wide / length[:, None]).astype(jnp.bfloat16), length)


def unit_back(grad, unit, length):
    wide = unit.astype(jnp.float32)
    along = jnp.sum(wide * grad, axis=1, keepdims=True)
    return (grad - wide * along) / length[:, None]


def pair_dot(left, right):
    return lax.dot_general(
        left, right, (((1,), (1,)), ((), ())), preferred_element_type=jnp.float32
    )


def across_slots(stack):
    return lax.psum(stack, "cols")


def exchange_sum(stack, axis, count):
    pieces = lax.all_to_all(stack.reshape(count, -1), axis, 0, 0)
    return jnp.sum(pieces, axis=0)


def exchange_gather(piece, axis, count, shape):
    copies = jnp.broadcast_to(piece.reshape(1, -1), (count, piece.size))
    return lax.all_to_all(copies, axis, 0, 0).reshape(shape)


def across_queries(stack, count):
    if stack.size % count == 0:
        return exchange_gather(exchange_sum(stack, "rows", count), "rows", count, stack.shape)
    if count & (count - 1):
        return lax.psum(stack, "rows")
    step = 1
    while step < count:
        pairs = [(i, i ^ step) for i in range(count)]
        stack = stack + lax.ppermute(stack, "rows", pairs)
        step *= 2
    return stack


def halving_scatter(block, axis, count):
    where = lax.axis_index(axis)
    step = count // 2
    while step >= 1:
        half = block.shape[0] // 2
        bit = (where // step) % 2
        keep = lax.dynamic_slice_in_dim(block, bit * half, half, 0)
        send = lax.dynamic_slice_in_dim(block, (1 - bit) * half, half, 0)
        pairs = [(i, i ^ step) for i in range(count)]
        block = keep + lax.ppermute(send, axis, pairs)
        step //= 2
    return block


def butterfly(block, axis, count, order):
    where = lax.axis_index(axis)
    for step in order:
        half = block.shape[0] // 2
        bit = (where // step) % 2
        keep = lax.dynamic_slice_in_dim(block, bit * half, half, 0)
        send = lax.dynamic_slice_in_dim(block, (1 - bit) * half, half, 0)
        pairs = [(i, i ^ step) for i in range(count)]
        block = keep + lax.ppermute(send, axis, pairs)
    for step in reversed(order):
        bit = (where // step) % 2
        pairs = [(i, i ^ step) for i in range(count)]
        other = lax.ppermute(block, axis, pairs)
        block = jnp.where(bit == 0, jnp.concatenate([block, other]), jnp.concatenate([other, block]))
    return block


def whole_sum(block, count, inner):
    bits = [1 << k for k in range(count.bit_length() - 1)]
    if count & (count - 1) or inner >= count or block.shape[0] % (2 * count):
        return lax.psum(block, "rows")
    low = [b for b in bits if b < inner]
    high = [b for b in bits if b >= inner]
    half = block.shape[0] // 2
    first = butterfly(block[:half], "rows", count, low + high)
    second = butterfly(block[half:], "rows", count, high + low)
    return jnp.concatenate([first, second])


def local(count, inner, width_cols, queries, prototypes, potential, weights, capacity, cotangent):
    qhat, qlen = unit_rows(queries)
    phat, plen = unit_rows(prototypes)
    wgt = weights.astype(jnp.float32)
    scaled = (cotangent.astype(jnp.float32) / wgt[:, None]).astype(jnp.bfloat16)
    local_rows = qhat.shape[0]
    slots = phat.shape[0]
    width = math.gcd(slots, 512)
    starts = list(range(0, slots, width))

    def kernel_tile(start):
        scores = pair_dot(qhat, phat[start : start + width])
        weight_cols = capacity[start : start + width].astype(jnp.float32)
        return weight_cols[None, :] * jnp.exp(
            (scores - potential[start : start + width][None, :]) / TEMPER
        )

    def coupling_tile(start):
        return pair_dot(scaled, phat[start : start + width])

    ztot = jnp.zeros((local_rows,), jnp.float32)
    kgsum = jnp.zeros((local_rows,), jnp.float32)
    for start in starts:
        kern = kernel_tile(start)
        ztot = ztot + jnp.sum(kern, axis=1)
        kgsum = kgsum + jnp.sum(kern * coupling_tile(start), axis=1)
    totals = across_slots(jnp.stack([ztot, kgsum]))
    share = wgt / totals[0]
    pvec = share * totals[1]
    alpha_one = pvec / wgt
    col_parts, q_parts, t_parts = ([], [], [])
    for start in starts:
        plan = share[:, None] * kernel_tile(start)
        col_parts.append(jnp.sum(plan, axis=0))
        q_parts.append(jnp.sum(plan * coupling_tile(start), axis=0))
    for start in starts:
        plan = share[:, None] * kernel_tile(start)
        t_parts.append(jnp.sum(alpha_one[:, None] * plan, axis=0))
    summed = across_queries(
        jnp.stack([jnp.concatenate(col_parts), jnp.concatenate(q_parts), jnp.concatenate(t_parts)]),
        count,
    )
    colsum, qvec, t_one = (summed[0], summed[1], summed[2])
    beta_one = (qvec - t_one) / colsum
    rowprod = jnp.zeros((local_rows,), jnp.float32)
    for start in starts:
        plan = share[:, None] * kernel_tile(start)
        rowprod = rowprod + jnp.sum(plan * beta_one[start : start + width][None, :], axis=1)
    rowprod = across_slots(rowprod[None, :])[0]
    alpha_two = (pvec - rowprod) / wgt
    t_parts = []
    for start in starts:
        plan = share[:, None] * kernel_tile(start)
        t_parts.append(jnp.sum(alpha_two[:, None] * plan, axis=0))
    t_two = across_queries(jnp.concatenate(t_parts)[None, :], count)[0]
    beta_two = (qvec - t_two) / colsum
    dqhat = jnp.zeros(qhat.shape, jnp.float32)
    dp_parts = []
    for start in starts:
        plan = share[:, None] * kernel_tile(start)
        coupling = coupling_tile(start)
        shift_cols = beta_two[start : start + width][None, :]
        dscore = (plan * (coupling - alpha_two[:, None] - shift_cols) / TEMPER).astype(jnp.bfloat16)
        planb = plan.astype(jnp.bfloat16)
        dqhat = dqhat + jnp.dot(
            dscore, phat[start : start + width], preferred_element_type=jnp.float32
        )
        part = lax.dot_general(
            dscore, qhat, (((0,), (0,)), ((), ())), preferred_element_type=jnp.float32
        )
        part = part + lax.dot_general(
            planb, scaled, (((0,), (0,)), ((), ())), preferred_element_type=jnp.float32
        )
        dp_parts.append(part)
    dphat = jnp.concatenate(dp_parts, axis=0)
    if local_rows % width_cols:
        query_part = lax.psum_scatter(dqhat, "cols", scatter_dimension=0, tiled=True)
    else:
        query_part = exchange_sum(dqhat, "cols", width_cols).reshape(-1, dqhat.shape[1])
    piece = query_part.shape[0]
    begin = lax.axis_index("cols") * piece
    grad_queries = unit_back(
        query_part,
        lax.dynamic_slice_in_dim(qhat, begin, piece, 0),
        lax.dynamic_slice_in_dim(qlen, begin, piece, 0),
    )
    if slots % count:
        grad_protos = unit_back(whole_sum(dphat, count, inner), phat, plen)
    else:
        own = slots // count
        first = lax.axis_index("rows") * own
        summed = exchange_sum(dphat, "rows", count).reshape(own, dphat.shape[1])
        piece = unit_back(
            summed,
            lax.dynamic_slice_in_dim(phat, first, own, 0),
            lax.dynamic_slice_in_dim(plen, first, own, 0),
        )
        grad_protos = exchange_gather(piece, "rows", count, dphat.shape)
    return (grad_queries, grad_protos)


def inner_of(mesh):
    column = list(mesh.devices[:, 0])
    try:
        lead = column[0].coords[1]
        return sum(1 for _ in itertools.takewhile(lambda d: d.coords[1] == lead, column))
    except (AttributeError, IndexError):
        return len(column)


def solution(mesh):
    in_specs = (P("rows", None), P("cols", None), P("cols"), P("rows"), P("cols"), P("rows", None))
    out_specs = (P(("rows", "cols"), None), P("cols", None))
    body = functools.partial(local, mesh.shape["rows"], inner_of(mesh), mesh.shape["cols"])
    return jax.shard_map(body, mesh=mesh, in_specs=in_specs, out_specs=out_specs, check_vma=False)
```

```python
import functools
import itertools
import math

import jax
import jax.numpy as jnp
from jax import lax
from jax.sharding import PartitionSpec as P

TEMPER = 0.05


def unit_rows(matrix):
    wide = matrix.astype(jnp.float32)
    length = jnp.sqrt(jnp.sum(wide * wide, axis=1) + 1e-06)
    return ((wide / length[:, None]).astype(jnp.bfloat16), length)


def unit_back(grad, unit, length):
    wide = unit.astype(jnp.float32)
    along = jnp.sum(wide * grad, axis=1, keepdims=True)
    return (grad - wide * along) / length[:, None]


def pair_dot(left, right):
    return lax.dot_general(
        left, right, (((1,), (1,)), ((), ())), preferred_element_type=jnp.float32
    )


def across_slots(stack):
    return lax.psum(stack, "cols")


def exchange_sum(stack, axis, count):
    pieces = lax.all_to_all(stack.reshape(count, -1), axis, 0, 0)
    return jnp.sum(pieces, axis=0)


def exchange_gather(piece, axis, count, shape):
    copies = jnp.broadcast_to(piece.reshape(1, -1), (count, piece.size))
    return lax.all_to_all(copies, axis, 0, 0).reshape(shape)


def across_queries(stack, count):
    if stack.size % count == 0:
        return exchange_gather(exchange_sum(stack, "rows", count), "rows", count, stack.shape)
    if count & (count - 1):
        return lax.psum(stack, "rows")
    step = 1
    while step < count:
        pairs = [(i, i ^ step) for i in range(count)]
        stack = stack + lax.ppermute(stack, "rows", pairs)
        step *= 2
    return stack


def halving_scatter(block, axis, count):
    where = lax.axis_index(axis)
    step = count // 2
    while step >= 1:
        half = block.shape[0] // 2
        bit = (where // step) % 2
        keep = lax.dynamic_slice_in_dim(block, bit * half, half, 0)
        send = lax.dynamic_slice_in_dim(block, (1 - bit) * half, half, 0)
        pairs = [(i, i ^ step) for i in range(count)]
        block = keep + lax.ppermute(send, axis, pairs)
        step //= 2
    return block


def butterfly(block, axis, count, order):
    where = lax.axis_index(axis)
    for step in order:
        half = block.shape[0] // 2
        bit = (where // step) % 2
        keep = lax.dynamic_slice_in_dim(block, bit * half, half, 0)
        send = lax.dynamic_slice_in_dim(block, (1 - bit) * half, half, 0)
        pairs = [(i, i ^ step) for i in range(count)]
        block = keep + lax.ppermute(send, axis, pairs)
    for step in reversed(order):
        bit = (where // step) % 2
        pairs = [(i, i ^ step) for i in range(count)]
        other = lax.ppermute(block, axis, pairs)
        block = jnp.where(bit == 0, jnp.concatenate([block, other]), jnp.concatenate([other, block]))
    return block


def whole_sum(block, count, inner):
    bits = [1 << k for k in range(count.bit_length() - 1)]
    if count & (count - 1) or inner >= count or block.shape[0] % (2 * count):
        return lax.psum(block, "rows")
    low = [b for b in bits if b < inner]
    high = [b for b in bits if b >= inner]
    half = block.shape[0] // 2
    first = butterfly(block[:half], "rows", count, low + high)
    second = butterfly(block[half:], "rows", count, high + low)
    return jnp.concatenate([first, second])


def local(count, inner, width_cols, queries, prototypes, potential, weights, capacity, cotangent):
    qhat, qlen = unit_rows(queries)
    phat, plen = unit_rows(prototypes)
    wgt = weights.astype(jnp.float32)
    scaled = (cotangent.astype(jnp.float32) / wgt[:, None]).astype(jnp.bfloat16)
    local_rows = qhat.shape[0]
    slots = phat.shape[0]
    width = math.gcd(slots, 512)
    starts = list(range(0, slots, width))

    def kernel_tile(start):
        scores = pair_dot(qhat, phat[start : start + width])
        weight_cols = capacity[start : start + width].astype(jnp.float32)
        return weight_cols[None, :] * jnp.exp(
            (scores - potential[start : start + width][None, :]) / TEMPER
        )

    def coupling_tile(start):
        return pair_dot(scaled, phat[start : start + width])

    ztot = jnp.zeros((local_rows,), jnp.float32)
    kgsum = jnp.zeros((local_rows,), jnp.float32)
    for start in starts:
        kern = kernel_tile(start)
        ztot = ztot + jnp.sum(kern, axis=1)
        kgsum = kgsum + jnp.sum(kern * coupling_tile(start), axis=1)
    totals = across_slots(jnp.stack([ztot, kgsum]))
    share = wgt / totals[0]
    pvec = share * totals[1]
    alpha_one = pvec / wgt
    col_parts, q_parts, t_parts = ([], [], [])
    for start in starts:
        plan = share[:, None] * kernel_tile(start)
        col_parts.append(jnp.sum(plan, axis=0))
        q_parts.append(jnp.sum(plan * coupling_tile(start), axis=0))
    for start in starts:
        plan = share[:, None] * kernel_tile(start)
        t_parts.append(jnp.sum(alpha_one[:, None] * plan, axis=0))
    summed = across_queries(
        jnp.stack([jnp.concatenate(col_parts), jnp.concatenate(q_parts), jnp.concatenate(t_parts)]),
        count,
    )
    colsum, qvec, t_one = (summed[0], summed[1], summed[2])
    beta_one = (qvec - t_one) / colsum
    rowprod = jnp.zeros((local_rows,), jnp.float32)
    for start in starts:
        plan = share[:, None] * kernel_tile(start)
        rowprod = rowprod + jnp.sum(plan * beta_one[start : start + width][None, :], axis=1)
    rowprod = across_slots(rowprod[None, :])[0]
    alpha_two = (pvec - rowprod) / wgt
    t_parts = []
    for start in starts:
        plan = share[:, None] * kernel_tile(start)
        t_parts.append(jnp.sum(alpha_two[:, None] * plan, axis=0))
    t_two = across_queries(jnp.concatenate(t_parts)[None, :], count)[0]
    beta_two = (qvec - t_two) / colsum
    dqhat = jnp.zeros(qhat.shape, jnp.float32)
    dp_parts = []
    for start in starts:
        plan = share[:, None] * kernel_tile(start)
        coupling = coupling_tile(start)
        shift_cols = beta_two[start : start + width][None, :]
        dscore = (plan * (coupling - alpha_two[:, None] - shift_cols) / TEMPER).astype(jnp.bfloat16)
        planb = plan.astype(jnp.bfloat16)
        dqhat = dqhat + jnp.dot(
            dscore, phat[start : start + width], preferred_element_type=jnp.float32
        )
        part = lax.dot_general(
            dscore, qhat, (((0,), (0,)), ((), ())), preferred_element_type=jnp.float32
        )
        part = part + lax.dot_general(
            planb, scaled, (((0,), (0,)), ((), ())), preferred_element_type=jnp.float32
        )
        dp_parts.append(part)
    dphat = jnp.concatenate(dp_parts, axis=0)
    if local_rows % width_cols:
        query_part = lax.psum_scatter(dqhat, "cols", scatter_dimension=0, tiled=True)
    else:
        query_part = halving_scatter(dqhat, "cols", width_cols)
    piece = query_part.shape[0]
    begin = lax.axis_index("cols") * piece
    grad_queries = unit_back(
        query_part,
        lax.dynamic_slice_in_dim(qhat, begin, piece, 0),
        lax.dynamic_slice_in_dim(qlen, begin, piece, 0),
    )
    if slots % count:
        grad_protos = unit_back(whole_sum(dphat, count, inner), phat, plen)
    else:
        own = slots // count
        first = lax.axis_index("rows") * own
        summed = exchange_sum(dphat, "rows", count).reshape(own, dphat.shape[1])
        piece = unit_back(
            summed,
            lax.dynamic_slice_in_dim(phat, first, own, 0),
            lax.dynamic_slice_in_dim(plen, first, own, 0),
        )
        grad_protos = exchange_gather(piece, "rows", count, dphat.shape)
    return (grad_queries, grad_protos)


def inner_of(mesh):
    column = list(mesh.devices[:, 0])
    try:
        lead = column[0].coords[1]
        return sum(1 for _ in itertools.takewhile(lambda d: d.coords[1] == lead, column))
    except (AttributeError, IndexError):
        return len(column)


def solution(mesh):
    in_specs = (P("rows", None), P("cols", None), P("cols"), P("rows"), P("cols"), P("rows", None))
    out_specs = (P(("rows", "cols"), None), P("cols", None))
    body = functools.partial(local, mesh.shape["rows"], inner_of(mesh), mesh.shape["cols"])
    return jax.shard_map(body, mesh=mesh, in_specs=in_specs, out_specs=out_specs, check_vma=False)
```

```python
import functools
import itertools
import math

import jax
import jax.numpy as jnp
from jax import lax
from jax.sharding import Mesh, PartitionSpec as P

TEMPER = 0.05


def unit_rows(matrix):
    wide = matrix.astype(jnp.float32)
    length = jnp.sqrt(jnp.sum(wide * wide, axis=1) + 1e-06)
    return ((wide / length[:, None]).astype(jnp.bfloat16), length)


def unit_back(grad, unit, length):
    wide = unit.astype(jnp.float32)
    along = jnp.sum(wide * grad, axis=1, keepdims=True)
    return (grad - wide * along) / length[:, None]


def pair_dot(left, right):
    return lax.dot_general(
        left, right, (((1,), (1,)), ((), ())), preferred_element_type=jnp.float32
    )


COLS = ("chips", "core")


def across_slots(stack):
    return lax.psum(lax.psum(stack, "core"), "chips")


def exchange_sum(stack, axis, count):
    pieces = lax.all_to_all(stack.reshape(count, -1), axis, 0, 0)
    return jnp.sum(pieces, axis=0)


def exchange_gather(piece, axis, count, shape):
    copies = jnp.broadcast_to(piece.reshape(1, -1), (count, piece.size))
    return lax.all_to_all(copies, axis, 0, 0).reshape(shape)


def across_queries(stack, count):
    if stack.size % count == 0:
        return exchange_gather(exchange_sum(stack, "rows", count), "rows", count, stack.shape)
    if count & (count - 1):
        return lax.psum(stack, "rows")
    step = 1
    while step < count:
        pairs = [(i, i ^ step) for i in range(count)]
        stack = stack + lax.ppermute(stack, "rows", pairs)
        step *= 2
    return stack


def halving_scatter(block, axis, count):
    where = lax.axis_index(axis)
    step = count // 2
    while step >= 1:
        half = block.shape[0] // 2
        bit = (where // step) % 2
        keep = lax.dynamic_slice_in_dim(block, bit * half, half, 0)
        send = lax.dynamic_slice_in_dim(block, (1 - bit) * half, half, 0)
        pairs = [(i, i ^ step) for i in range(count)]
        block = keep + lax.ppermute(send, axis, pairs)
        step //= 2
    return block


def butterfly(block, axis, count, order):
    where = lax.axis_index(axis)
    for step in order:
        half = block.shape[0] // 2
        bit = (where // step) % 2
        keep = lax.dynamic_slice_in_dim(block, bit * half, half, 0)
        send = lax.dynamic_slice_in_dim(block, (1 - bit) * half, half, 0)
        pairs = [(i, i ^ step) for i in range(count)]
        block = keep + lax.ppermute(send, axis, pairs)
    for step in reversed(order):
        bit = (where // step) % 2
        pairs = [(i, i ^ step) for i in range(count)]
        other = lax.ppermute(block, axis, pairs)
        block = jnp.where(bit == 0, jnp.concatenate([block, other]), jnp.concatenate([other, block]))
    return block


def whole_sum(block, count, inner):
    bits = [1 << k for k in range(count.bit_length() - 1)]
    if count & (count - 1) or inner >= count or block.shape[0] % (2 * count):
        return lax.psum(block, "rows")
    low = [b for b in bits if b < inner]
    high = [b for b in bits if b >= inner]
    half = block.shape[0] // 2
    first = butterfly(block[:half], "rows", count, low + high)
    second = butterfly(block[half:], "rows", count, high + low)
    return jnp.concatenate([first, second])


def local(count, inner, width_cols, queries, prototypes, potential, weights, capacity, cotangent):
    qhat, qlen = unit_rows(queries)
    phat, plen = unit_rows(prototypes)
    wgt = weights.astype(jnp.float32)
    scaled = (cotangent.astype(jnp.float32) / wgt[:, None]).astype(jnp.bfloat16)
    local_rows = qhat.shape[0]
    slots = phat.shape[0]
    width = math.gcd(slots, 512)
    starts = list(range(0, slots, width))

    def kernel_tile(start):
        scores = pair_dot(qhat, phat[start : start + width])
        weight_cols = capacity[start : start + width].astype(jnp.float32)
        return weight_cols[None, :] * jnp.exp(
            (scores - potential[start : start + width][None, :]) / TEMPER
        )

    def coupling_tile(start):
        return pair_dot(scaled, phat[start : start + width])

    ztot = jnp.zeros((local_rows,), jnp.float32)
    kgsum = jnp.zeros((local_rows,), jnp.float32)
    for start in starts:
        kern = kernel_tile(start)
        ztot = ztot + jnp.sum(kern, axis=1)
        kgsum = kgsum + jnp.sum(kern * coupling_tile(start), axis=1)
    totals = across_slots(jnp.stack([ztot, kgsum]))
    share = wgt / totals[0]
    pvec = share * totals[1]
    alpha_one = pvec / wgt
    col_parts, q_parts, t_parts = ([], [], [])
    for start in starts:
        plan = share[:, None] * kernel_tile(start)
        col_parts.append(jnp.sum(plan, axis=0))
        q_parts.append(jnp.sum(plan * coupling_tile(start), axis=0))
    for start in starts:
        plan = share[:, None] * kernel_tile(start)
        t_parts.append(jnp.sum(alpha_one[:, None] * plan, axis=0))
    summed = across_queries(
        jnp.stack([jnp.concatenate(col_parts), jnp.concatenate(q_parts), jnp.concatenate(t_parts)]),
        count,
    )
    colsum, qvec, t_one = (summed[0], summed[1], summed[2])
    beta_one = (qvec - t_one) / colsum
    rowprod = jnp.zeros((local_rows,), jnp.float32)
    for start in starts:
        plan = share[:, None] * kernel_tile(start)
        rowprod = rowprod + jnp.sum(plan * beta_one[start : start + width][None, :], axis=1)
    rowprod = across_slots(rowprod[None, :])[0]
    alpha_two = (pvec - rowprod) / wgt
    t_parts = []
    for start in starts:
        plan = share[:, None] * kernel_tile(start)
        t_parts.append(jnp.sum(alpha_two[:, None] * plan, axis=0))
    t_two = across_queries(jnp.concatenate(t_parts)[None, :], count)[0]
    beta_two = (qvec - t_two) / colsum
    dqhat = jnp.zeros(qhat.shape, jnp.float32)
    dp_parts = []
    for start in starts:
        plan = share[:, None] * kernel_tile(start)
        coupling = coupling_tile(start)
        shift_cols = beta_two[start : start + width][None, :]
        dscore = (plan * (coupling - alpha_two[:, None] - shift_cols) / TEMPER).astype(jnp.bfloat16)
        planb = plan.astype(jnp.bfloat16)
        dqhat = dqhat + jnp.dot(
            dscore, phat[start : start + width], preferred_element_type=jnp.float32
        )
        part = lax.dot_general(
            dscore, qhat, (((0,), (0,)), ((), ())), preferred_element_type=jnp.float32
        )
        part = part + lax.dot_general(
            planb, scaled, (((0,), (0,)), ((), ())), preferred_element_type=jnp.float32
        )
        dp_parts.append(part)
    dphat = jnp.concatenate(dp_parts, axis=0)
    if local_rows % width_cols:
        query_part = lax.psum_scatter(dqhat, COLS, scatter_dimension=0, tiled=True)
    else:
        query_part = halving_scatter(dqhat, COLS, width_cols)
    piece = query_part.shape[0]
    begin = lax.axis_index(COLS) * piece
    grad_queries = unit_back(
        query_part,
        lax.dynamic_slice_in_dim(qhat, begin, piece, 0),
        lax.dynamic_slice_in_dim(qlen, begin, piece, 0),
    )
    if slots % count:
        grad_protos = unit_back(whole_sum(dphat, count, inner), phat, plen)
    else:
        own = slots // count
        first = lax.axis_index("rows") * own
        summed = exchange_sum(dphat, "rows", count).reshape(own, dphat.shape[1])
        piece = unit_back(
            summed,
            lax.dynamic_slice_in_dim(phat, first, own, 0),
            lax.dynamic_slice_in_dim(plen, first, own, 0),
        )
        grad_protos = exchange_gather(piece, "rows", count, dphat.shape)
    return (grad_queries, grad_protos)


def inner_of(mesh):
    column = list(mesh.devices[:, 0])
    try:
        lead = column[0].coords[1]
        return sum(1 for _ in itertools.takewhile(lambda d: d.coords[1] == lead, column))
    except (AttributeError, IndexError):
        return len(column)


def cores_of(mesh):
    row = list(mesh.devices[0, :])
    try:
        lead = row[0].coords
        return sum(1 for _ in itertools.takewhile(lambda d: d.coords == lead, row))
    except AttributeError:
        return 1


def solution(mesh):
    rows, cols = mesh.shape["rows"], mesh.shape["cols"]
    cores = cores_of(mesh)
    if cols % cores:
        cores = 1
    grid = Mesh(mesh.devices.reshape(rows, cols // cores, cores), ("rows",) + COLS)
    in_specs = (P("rows", None), P(COLS, None), P(COLS), P("rows"), P(COLS), P("rows", None))
    out_specs = (P(("rows",) + COLS, None), P(COLS, None))
    body = functools.partial(local, rows, inner_of(mesh), cols)
    return jax.shard_map(body, mesh=grid, in_specs=in_specs, out_specs=out_specs, check_vma=False)
```

```python
import functools
import itertools
import math

import jax
import jax.numpy as jnp
from jax import lax
from jax.sharding import Mesh, PartitionSpec as P

TEMPER = 0.05


def unit_rows(matrix):
    wide = matrix.astype(jnp.float32)
    length = jnp.sqrt(jnp.sum(wide * wide, axis=1) + 1e-06)
    return ((wide / length[:, None]).astype(jnp.bfloat16), length)


def unit_back(grad, unit, length):
    wide = unit.astype(jnp.float32)
    along = jnp.sum(wide * grad, axis=1, keepdims=True)
    return (grad - wide * along) / length[:, None]


def pair_dot(left, right):
    return lax.dot_general(
        left, right, (((1,), (1,)), ((), ())), preferred_element_type=jnp.float32
    )


COLS = ("chips", "core")


def across_slots(stack):
    return lax.psum(lax.psum(stack, "core"), "chips")


def exchange_sum(stack, axis, count):
    pieces = lax.all_to_all(stack.reshape(count, -1), axis, 0, 0)
    return jnp.sum(pieces, axis=0)


def exchange_gather(piece, axis, count, shape):
    copies = jnp.broadcast_to(piece.reshape(1, -1), (count, piece.size))
    return lax.all_to_all(copies, axis, 0, 0).reshape(shape)


def spread_sum(stack, axis, count):
    copies = jnp.broadcast_to(stack.reshape(1, -1), (count, stack.size))
    return jnp.sum(lax.all_to_all(copies, axis, 0, 0), axis=0).reshape(stack.shape)


def across_queries(stack, count, spread=False):
    if spread:
        return spread_sum(stack, "rows", count)
    if stack.size % count == 0:
        return exchange_gather(exchange_sum(stack, "rows", count), "rows", count, stack.shape)
    if count & (count - 1):
        return lax.psum(stack, "rows")
    step = 1
    while step < count:
        pairs = [(i, i ^ step) for i in range(count)]
        stack = stack + lax.ppermute(stack, "rows", pairs)
        step *= 2
    return stack


def halving_scatter(block, axis, count):
    where = lax.axis_index(axis)
    step = count // 2
    while step >= 1:
        half = block.shape[0] // 2
        bit = (where // step) % 2
        keep = lax.dynamic_slice_in_dim(block, bit * half, half, 0)
        send = lax.dynamic_slice_in_dim(block, (1 - bit) * half, half, 0)
        pairs = [(i, i ^ step) for i in range(count)]
        block = keep + lax.ppermute(send, axis, pairs)
        step //= 2
    return block


def butterfly(block, axis, count, order):
    where = lax.axis_index(axis)
    for step in order:
        half = block.shape[0] // 2
        bit = (where // step) % 2
        keep = lax.dynamic_slice_in_dim(block, bit * half, half, 0)
        send = lax.dynamic_slice_in_dim(block, (1 - bit) * half, half, 0)
        pairs = [(i, i ^ step) for i in range(count)]
        block = keep + lax.ppermute(send, axis, pairs)
    for step in reversed(order):
        bit = (where // step) % 2
        pairs = [(i, i ^ step) for i in range(count)]
        other = lax.ppermute(block, axis, pairs)
        block = jnp.where(bit == 0, jnp.concatenate([block, other]), jnp.concatenate([other, block]))
    return block


def whole_sum(block, count, inner):
    bits = [1 << k for k in range(count.bit_length() - 1)]
    if count & (count - 1) or inner >= count or block.shape[0] % (2 * count):
        return lax.psum(block, "rows")
    low = [b for b in bits if b < inner]
    high = [b for b in bits if b >= inner]
    half = block.shape[0] // 2
    first = butterfly(block[:half], "rows", count, low + high)
    second = butterfly(block[half:], "rows", count, high + low)
    return jnp.concatenate([first, second])


def local(count, inner, width_cols, queries, prototypes, potential, weights, capacity, cotangent):
    qhat, qlen = unit_rows(queries)
    phat, plen = unit_rows(prototypes)
    wgt = weights.astype(jnp.float32)
    scaled = (cotangent.astype(jnp.float32) / wgt[:, None]).astype(jnp.bfloat16)
    local_rows = qhat.shape[0]
    slots = phat.shape[0]
    width = math.gcd(slots, 512)
    starts = list(range(0, slots, width))

    def kernel_tile(start):
        scores = pair_dot(qhat, phat[start : start + width])
        weight_cols = capacity[start : start + width].astype(jnp.float32)
        return weight_cols[None, :] * jnp.exp(
            (scores - potential[start : start + width][None, :]) / TEMPER
        )

    def coupling_tile(start):
        return pair_dot(scaled, phat[start : start + width])

    ztot = jnp.zeros((local_rows,), jnp.float32)
    kgsum = jnp.zeros((local_rows,), jnp.float32)
    for start in starts:
        kern = kernel_tile(start)
        ztot = ztot + jnp.sum(kern, axis=1)
        kgsum = kgsum + jnp.sum(kern * coupling_tile(start), axis=1)
    totals = across_slots(jnp.stack([ztot, kgsum]))
    share = wgt / totals[0]
    pvec = share * totals[1]
    alpha_one = pvec / wgt
    col_parts, q_parts, t_parts = ([], [], [])
    for start in starts:
        plan = share[:, None] * kernel_tile(start)
        col_parts.append(jnp.sum(plan, axis=0))
        q_parts.append(jnp.sum(plan * coupling_tile(start), axis=0))
    for start in starts:
        plan = share[:, None] * kernel_tile(start)
        t_parts.append(jnp.sum(alpha_one[:, None] * plan, axis=0))
    summed = across_queries(
        jnp.stack([jnp.concatenate(col_parts), jnp.concatenate(q_parts), jnp.concatenate(t_parts)]),
        count,
    )
    colsum, qvec, t_one = (summed[0], summed[1], summed[2])
    beta_one = (qvec - t_one) / colsum
    rowprod = jnp.zeros((local_rows,), jnp.float32)
    for start in starts:
        plan = share[:, None] * kernel_tile(start)
        rowprod = rowprod + jnp.sum(plan * beta_one[start : start + width][None, :], axis=1)
    rowprod = across_slots(rowprod[None, :])[0]
    alpha_two = (pvec - rowprod) / wgt
    t_parts = []
    for start in starts:
        plan = share[:, None] * kernel_tile(start)
        t_parts.append(jnp.sum(alpha_two[:, None] * plan, axis=0))
    t_two = across_queries(jnp.concatenate(t_parts)[None, :], count, spread=True)[0]
    beta_two = (qvec - t_two) / colsum
    dqhat = jnp.zeros(qhat.shape, jnp.float32)
    dp_parts = []
    for start in starts:
        plan = share[:, None] * kernel_tile(start)
        coupling = coupling_tile(start)
        shift_cols = beta_two[start : start + width][None, :]
        dscore = (plan * (coupling - alpha_two[:, None] - shift_cols) / TEMPER).astype(jnp.bfloat16)
        planb = plan.astype(jnp.bfloat16)
        dqhat = dqhat + jnp.dot(
            dscore, phat[start : start + width], preferred_element_type=jnp.float32
        )
        part = lax.dot_general(
            dscore, qhat, (((0,), (0,)), ((), ())), preferred_element_type=jnp.float32
        )
        part = part + lax.dot_general(
            planb, scaled, (((0,), (0,)), ((), ())), preferred_element_type=jnp.float32
        )
        dp_parts.append(part)
    dphat = jnp.concatenate(dp_parts, axis=0)
    if local_rows % width_cols:
        query_part = lax.psum_scatter(dqhat, COLS, scatter_dimension=0, tiled=True)
    else:
        query_part = halving_scatter(dqhat, COLS, width_cols)
    piece = query_part.shape[0]
    begin = lax.axis_index(COLS) * piece
    grad_queries = unit_back(
        query_part,
        lax.dynamic_slice_in_dim(qhat, begin, piece, 0),
        lax.dynamic_slice_in_dim(qlen, begin, piece, 0),
    )
    if slots % count:
        grad_protos = unit_back(whole_sum(dphat, count, inner), phat, plen)
    else:
        own = slots // count
        first = lax.axis_index("rows") * own
        summed = exchange_sum(dphat, "rows", count).reshape(own, dphat.shape[1])
        piece = unit_back(
            summed,
            lax.dynamic_slice_in_dim(phat, first, own, 0),
            lax.dynamic_slice_in_dim(plen, first, own, 0),
        )
        grad_protos = exchange_gather(piece, "rows", count, dphat.shape)
    return (grad_queries, grad_protos)


def inner_of(mesh):
    column = list(mesh.devices[:, 0])
    try:
        lead = column[0].coords[1]
        return sum(1 for _ in itertools.takewhile(lambda d: d.coords[1] == lead, column))
    except (AttributeError, IndexError):
        return len(column)


def cores_of(mesh):
    row = list(mesh.devices[0, :])
    try:
        lead = row[0].coords
        return sum(1 for _ in itertools.takewhile(lambda d: d.coords == lead, row))
    except AttributeError:
        return 1


def solution(mesh):
    rows, cols = mesh.shape["rows"], mesh.shape["cols"]
    cores = cores_of(mesh)
    if cols % cores:
        cores = 1
    grid = Mesh(mesh.devices.reshape(rows, cols // cores, cores), ("rows",) + COLS)
    in_specs = (P("rows", None), P(COLS, None), P(COLS), P("rows"), P(COLS), P("rows", None))
    out_specs = (P(("rows",) + COLS, None), P(COLS, None))
    body = functools.partial(local, rows, inner_of(mesh), cols)
    return jax.shard_map(body, mesh=grid, in_specs=in_specs, out_specs=out_specs, check_vma=False)
```

```python
import functools
import itertools
import math

import jax
import jax.numpy as jnp
from jax import lax
from jax.sharding import Mesh, PartitionSpec as P

TEMPER = 0.05


def unit_rows(matrix):
    wide = matrix.astype(jnp.float32)
    length = jnp.sqrt(jnp.sum(wide * wide, axis=1) + 1e-06)
    return ((wide / length[:, None]).astype(jnp.bfloat16), length)


def unit_back(grad, unit, length):
    wide = unit.astype(jnp.float32)
    along = jnp.sum(wide * grad, axis=1, keepdims=True)
    return (grad - wide * along) / length[:, None]


def pair_dot(left, right):
    return lax.dot_general(
        left, right, (((1,), (1,)), ((), ())), preferred_element_type=jnp.float32
    )


COLS = ("chips", "core")


def across_slots(stack):
    return lax.psum(lax.psum(stack, "core"), "chips")


def exchange_sum(stack, axis, count):
    pieces = lax.all_to_all(stack.reshape(count, -1), axis, 0, 0)
    return jnp.sum(pieces, axis=0)


def exchange_gather(piece, axis, count, shape):
    copies = jnp.broadcast_to(piece.reshape(1, -1), (count, piece.size))
    return lax.all_to_all(copies, axis, 0, 0).reshape(shape)


def spread_sum(stack, axis, count):
    copies = jnp.broadcast_to(stack.reshape(1, -1), (count, stack.size))
    return jnp.sum(lax.all_to_all(copies, axis, 0, 0), axis=0).reshape(stack.shape)


def across_queries(stack, count, spread=False):
    if spread:
        return spread_sum(stack, "rows", count)
    if stack.size % count == 0:
        return exchange_gather(exchange_sum(stack, "rows", count), "rows", count, stack.shape)
    if count & (count - 1):
        return lax.psum(stack, "rows")
    step = 1
    while step < count:
        pairs = [(i, i ^ step) for i in range(count)]
        stack = stack + lax.ppermute(stack, "rows", pairs)
        step *= 2
    return stack


def halving_scatter(block, axis, count):
    where = lax.axis_index(axis)
    step = count // 2
    while step >= 1:
        half = block.shape[0] // 2
        bit = (where // step) % 2
        keep = lax.dynamic_slice_in_dim(block, bit * half, half, 0)
        send = lax.dynamic_slice_in_dim(block, (1 - bit) * half, half, 0)
        pairs = [(i, i ^ step) for i in range(count)]
        block = keep + lax.ppermute(send, axis, pairs)
        step //= 2
    return block


def butterfly(block, axis, count, order):
    where = lax.axis_index(axis)
    for step in order:
        half = block.shape[0] // 2
        bit = (where // step) % 2
        keep = lax.dynamic_slice_in_dim(block, bit * half, half, 0)
        send = lax.dynamic_slice_in_dim(block, (1 - bit) * half, half, 0)
        pairs = [(i, i ^ step) for i in range(count)]
        block = keep + lax.ppermute(send, axis, pairs)
    for step in reversed(order):
        bit = (where // step) % 2
        pairs = [(i, i ^ step) for i in range(count)]
        other = lax.ppermute(block, axis, pairs)
        block = jnp.where(bit == 0, jnp.concatenate([block, other]), jnp.concatenate([other, block]))
    return block


def whole_sum(block, count, inner):
    bits = [1 << k for k in range(count.bit_length() - 1)]
    if count & (count - 1) or inner >= count or block.shape[0] % (2 * count):
        return lax.psum(block, "rows")
    low = [b for b in bits if b < inner]
    high = [b for b in bits if b >= inner]
    half = block.shape[0] // 2
    first = butterfly(block[:half], "rows", count, low + high)
    second = butterfly(block[half:], "rows", count, high + low)
    return jnp.concatenate([first, second])


def local(count, inner, width_cols, queries, prototypes, potential, weights, capacity, cotangent):
    qhat, qlen = unit_rows(queries)
    phat, plen = unit_rows(prototypes)
    wgt = weights.astype(jnp.float32)
    scaled = (cotangent.astype(jnp.float32) / wgt[:, None]).astype(jnp.bfloat16)
    local_rows = qhat.shape[0]
    slots = phat.shape[0]
    width = math.gcd(slots, 512)
    starts = list(range(0, slots, width))

    def kernel_tile(start):
        scores = pair_dot(qhat, phat[start : start + width])
        weight_cols = capacity[start : start + width].astype(jnp.float32)
        return weight_cols[None, :] * jnp.exp(
            (scores - potential[start : start + width][None, :]) / TEMPER
        )

    def coupling_tile(start):
        return pair_dot(scaled, phat[start : start + width])

    ztot = jnp.zeros((local_rows,), jnp.float32)
    kgsum = jnp.zeros((local_rows,), jnp.float32)
    for start in starts:
        kern = kernel_tile(start)
        ztot = ztot + jnp.sum(kern, axis=1)
        kgsum = kgsum + jnp.sum(kern * coupling_tile(start), axis=1)
    totals = across_slots(jnp.stack([ztot, kgsum]))
    share = wgt / totals[0]
    pvec = share * totals[1]
    alpha_one = pvec / wgt
    col_parts, q_parts, t_parts = ([], [], [])
    for start in starts:
        plan = share[:, None] * kernel_tile(start)
        col_parts.append(jnp.sum(plan, axis=0))
        q_parts.append(jnp.sum(plan * coupling_tile(start), axis=0))
    for start in starts:
        plan = share[:, None] * kernel_tile(start)
        t_parts.append(jnp.sum(alpha_one[:, None] * plan, axis=0))
    summed = across_queries(
        jnp.stack([jnp.concatenate(col_parts), jnp.concatenate(q_parts), jnp.concatenate(t_parts)]),
        count,
        spread=True,
    )
    colsum, qvec, t_one = (summed[0], summed[1], summed[2])
    beta_one = (qvec - t_one) / colsum
    rowprod = jnp.zeros((local_rows,), jnp.float32)
    for start in starts:
        plan = share[:, None] * kernel_tile(start)
        rowprod = rowprod + jnp.sum(plan * beta_one[start : start + width][None, :], axis=1)
    rowprod = across_slots(rowprod[None, :])[0]
    alpha_two = (pvec - rowprod) / wgt
    t_parts = []
    for start in starts:
        plan = share[:, None] * kernel_tile(start)
        t_parts.append(jnp.sum(alpha_two[:, None] * plan, axis=0))
    t_two = across_queries(jnp.concatenate(t_parts)[None, :], count, spread=True)[0]
    beta_two = (qvec - t_two) / colsum
    dqhat = jnp.zeros(qhat.shape, jnp.float32)
    dp_parts = []
    for start in starts:
        plan = share[:, None] * kernel_tile(start)
        coupling = coupling_tile(start)
        shift_cols = beta_two[start : start + width][None, :]
        dscore = (plan * (coupling - alpha_two[:, None] - shift_cols) / TEMPER).astype(jnp.bfloat16)
        planb = plan.astype(jnp.bfloat16)
        dqhat = dqhat + jnp.dot(
            dscore, phat[start : start + width], preferred_element_type=jnp.float32
        )
        part = lax.dot_general(
            dscore, qhat, (((0,), (0,)), ((), ())), preferred_element_type=jnp.float32
        )
        part = part + lax.dot_general(
            planb, scaled, (((0,), (0,)), ((), ())), preferred_element_type=jnp.float32
        )
        dp_parts.append(part)
    dphat = jnp.concatenate(dp_parts, axis=0)
    if local_rows % width_cols:
        query_part = lax.psum_scatter(dqhat, COLS, scatter_dimension=0, tiled=True)
    else:
        query_part = halving_scatter(dqhat, COLS, width_cols)
    piece = query_part.shape[0]
    begin = lax.axis_index(COLS) * piece
    grad_queries = unit_back(
        query_part,
        lax.dynamic_slice_in_dim(qhat, begin, piece, 0),
        lax.dynamic_slice_in_dim(qlen, begin, piece, 0),
    )
    if slots % count:
        grad_protos = unit_back(whole_sum(dphat, count, inner), phat, plen)
    else:
        own = slots // count
        first = lax.axis_index("rows") * own
        summed = exchange_sum(dphat, "rows", count).reshape(own, dphat.shape[1])
        piece = unit_back(
            summed,
            lax.dynamic_slice_in_dim(phat, first, own, 0),
            lax.dynamic_slice_in_dim(plen, first, own, 0),
        )
        grad_protos = exchange_gather(piece, "rows", count, dphat.shape)
    return (grad_queries, grad_protos)


def inner_of(mesh):
    column = list(mesh.devices[:, 0])
    try:
        lead = column[0].coords[1]
        return sum(1 for _ in itertools.takewhile(lambda d: d.coords[1] == lead, column))
    except (AttributeError, IndexError):
        return len(column)


def cores_of(mesh):
    row = list(mesh.devices[0, :])
    try:
        lead = row[0].coords
        return sum(1 for _ in itertools.takewhile(lambda d: d.coords == lead, row))
    except AttributeError:
        return 1


def solution(mesh):
    rows, cols = mesh.shape["rows"], mesh.shape["cols"]
    cores = cores_of(mesh)
    if cols % cores:
        cores = 1
    grid = Mesh(mesh.devices.reshape(rows, cols // cores, cores), ("rows",) + COLS)
    in_specs = (P("rows", None), P(COLS, None), P(COLS), P("rows"), P(COLS), P("rows", None))
    out_specs = (P(("rows",) + COLS, None), P(COLS, None))
    body = functools.partial(local, rows, inner_of(mesh), cols)
    return jax.shard_map(body, mesh=grid, in_specs=in_specs, out_specs=out_specs, check_vma=False)
```

```python
import functools
import itertools
import math

import jax
import jax.numpy as jnp
from jax import lax
from jax.sharding import Mesh, PartitionSpec as P

TEMPER = 0.05


def unit_rows(matrix):
    wide = matrix.astype(jnp.float32)
    length = jnp.sqrt(jnp.sum(wide * wide, axis=1) + 1e-06)
    return ((wide / length[:, None]).astype(jnp.bfloat16), length)


def unit_back(grad, unit, length):
    wide = unit.astype(jnp.float32)
    along = jnp.sum(wide * grad, axis=1, keepdims=True)
    return (grad - wide * along) / length[:, None]


def pair_dot(left, right):
    return lax.dot_general(
        left, right, (((1,), (1,)), ((), ())), preferred_element_type=jnp.float32
    )


COLS = ("chips", "core")
ROWS = ("slab", "lane")


def across_slots(stack):
    return lax.psum(lax.psum(stack, "core"), "chips")


def exchange_sum(stack, axis, count):
    pieces = lax.all_to_all(stack.reshape(count, -1), axis, 0, 0)
    return jnp.sum(pieces, axis=0)


def exchange_gather(piece, axis, count, shape):
    copies = jnp.broadcast_to(piece.reshape(1, -1), (count, piece.size))
    return lax.all_to_all(copies, axis, 0, 0).reshape(shape)


def spread_sum(stack, axis, count):
    copies = jnp.broadcast_to(stack.reshape(1, -1), (count, stack.size))
    return jnp.sum(lax.all_to_all(copies, axis, 0, 0), axis=0).reshape(stack.shape)


def across_queries(stack, count, inner, spread=False):
    if spread:
        return spread_sum(spread_sum(stack, "lane", inner), "slab", count // inner)
    if stack.size % count == 0:
        return exchange_gather(exchange_sum(stack, ROWS, count), ROWS, count, stack.shape)
    if count & (count - 1):
        return lax.psum(stack, ROWS)
    step = 1
    while step < count:
        pairs = [(i, i ^ step) for i in range(count)]
        stack = stack + lax.ppermute(stack, ROWS, pairs)
        step *= 2
    return stack


def halving_scatter(block, axis, count):
    where = lax.axis_index(axis)
    step = count // 2
    while step >= 1:
        half = block.shape[0] // 2
        bit = (where // step) % 2
        keep = lax.dynamic_slice_in_dim(block, bit * half, half, 0)
        send = lax.dynamic_slice_in_dim(block, (1 - bit) * half, half, 0)
        pairs = [(i, i ^ step) for i in range(count)]
        block = keep + lax.ppermute(send, axis, pairs)
        step //= 2
    return block


def butterfly(block, axis, count, order):
    where = lax.axis_index(axis)
    for step in order:
        half = block.shape[0] // 2
        bit = (where // step) % 2
        keep = lax.dynamic_slice_in_dim(block, bit * half, half, 0)
        send = lax.dynamic_slice_in_dim(block, (1 - bit) * half, half, 0)
        pairs = [(i, i ^ step) for i in range(count)]
        block = keep + lax.ppermute(send, axis, pairs)
    for step in reversed(order):
        bit = (where // step) % 2
        pairs = [(i, i ^ step) for i in range(count)]
        other = lax.ppermute(block, axis, pairs)
        block = jnp.where(bit == 0, jnp.concatenate([block, other]), jnp.concatenate([other, block]))
    return block


def whole_sum(block, count, inner):
    bits = [1 << k for k in range(count.bit_length() - 1)]
    if count & (count - 1) or inner >= count or block.shape[0] % (2 * count):
        return lax.psum(block, ROWS)
    low = [b for b in bits if b < inner]
    high = [b for b in bits if b >= inner]
    half = block.shape[0] // 2
    first = butterfly(block[:half], ROWS, count, low + high)
    second = butterfly(block[half:], ROWS, count, high + low)
    return jnp.concatenate([first, second])


def local(count, inner, width_cols, queries, prototypes, potential, weights, capacity, cotangent):
    qhat, qlen = unit_rows(queries)
    phat, plen = unit_rows(prototypes)
    wgt = weights.astype(jnp.float32)
    scaled = (cotangent.astype(jnp.float32) / wgt[:, None]).astype(jnp.bfloat16)
    local_rows = qhat.shape[0]
    slots = phat.shape[0]
    width = math.gcd(slots, 512)
    starts = list(range(0, slots, width))

    def kernel_tile(start):
        scores = pair_dot(qhat, phat[start : start + width])
        weight_cols = capacity[start : start + width].astype(jnp.float32)
        return weight_cols[None, :] * jnp.exp(
            (scores - potential[start : start + width][None, :]) / TEMPER
        )

    def coupling_tile(start):
        return pair_dot(scaled, phat[start : start + width])

    ztot = jnp.zeros((local_rows,), jnp.float32)
    kgsum = jnp.zeros((local_rows,), jnp.float32)
    for start in starts:
        kern = kernel_tile(start)
        ztot = ztot + jnp.sum(kern, axis=1)
        kgsum = kgsum + jnp.sum(kern * coupling_tile(start), axis=1)
    totals = across_slots(jnp.stack([ztot, kgsum]))
    share = wgt / totals[0]
    pvec = share * totals[1]
    alpha_one = pvec / wgt
    col_parts, q_parts, t_parts = ([], [], [])
    for start in starts:
        plan = share[:, None] * kernel_tile(start)
        col_parts.append(jnp.sum(plan, axis=0))
        q_parts.append(jnp.sum(plan * coupling_tile(start), axis=0))
    for start in starts:
        plan = share[:, None] * kernel_tile(start)
        t_parts.append(jnp.sum(alpha_one[:, None] * plan, axis=0))
    summed = across_queries(
        jnp.stack([jnp.concatenate(col_parts), jnp.concatenate(q_parts), jnp.concatenate(t_parts)]),
        count,
        inner,
        spread=True,
    )
    colsum, qvec, t_one = (summed[0], summed[1], summed[2])
    beta_one = (qvec - t_one) / colsum
    rowprod = jnp.zeros((local_rows,), jnp.float32)
    for start in starts:
        plan = share[:, None] * kernel_tile(start)
        rowprod = rowprod + jnp.sum(plan * beta_one[start : start + width][None, :], axis=1)
    rowprod = across_slots(rowprod[None, :])[0]
    alpha_two = (pvec - rowprod) / wgt
    t_parts = []
    for start in starts:
        plan = share[:, None] * kernel_tile(start)
        t_parts.append(jnp.sum(alpha_two[:, None] * plan, axis=0))
    t_two = across_queries(jnp.concatenate(t_parts)[None, :], count, inner, spread=True)[0]
    beta_two = (qvec - t_two) / colsum
    dqhat = jnp.zeros(qhat.shape, jnp.float32)
    dp_parts = []
    for start in starts:
        plan = share[:, None] * kernel_tile(start)
        coupling = coupling_tile(start)
        shift_cols = beta_two[start : start + width][None, :]
        dscore = (plan * (coupling - alpha_two[:, None] - shift_cols) / TEMPER).astype(jnp.bfloat16)
        planb = plan.astype(jnp.bfloat16)
        dqhat = dqhat + jnp.dot(
            dscore, phat[start : start + width], preferred_element_type=jnp.float32
        )
        part = lax.dot_general(
            dscore, qhat, (((0,), (0,)), ((), ())), preferred_element_type=jnp.float32
        )
        part = part + lax.dot_general(
            planb, scaled, (((0,), (0,)), ((), ())), preferred_element_type=jnp.float32
        )
        dp_parts.append(part)
    dphat = jnp.concatenate(dp_parts, axis=0)
    if local_rows % width_cols:
        query_part = lax.psum_scatter(dqhat, COLS, scatter_dimension=0, tiled=True)
    else:
        query_part = halving_scatter(dqhat, COLS, width_cols)
    piece = query_part.shape[0]
    begin = lax.axis_index(COLS) * piece
    grad_queries = unit_back(
        query_part,
        lax.dynamic_slice_in_dim(qhat, begin, piece, 0),
        lax.dynamic_slice_in_dim(qlen, begin, piece, 0),
    )
    if slots % count:
        grad_protos = unit_back(whole_sum(dphat, count, inner), phat, plen)
    else:
        own = slots // count
        first = lax.axis_index(ROWS) * own
        summed = exchange_sum(dphat, ROWS, count).reshape(own, dphat.shape[1])
        piece = unit_back(
            summed,
            lax.dynamic_slice_in_dim(phat, first, own, 0),
            lax.dynamic_slice_in_dim(plen, first, own, 0),
        )
        grad_protos = exchange_gather(piece, ROWS, count, dphat.shape)
    return (grad_queries, grad_protos)


def inner_of(mesh):
    column = list(mesh.devices[:, 0])
    try:
        lead = column[0].coords[1]
        return sum(1 for _ in itertools.takewhile(lambda d: d.coords[1] == lead, column))
    except (AttributeError, IndexError):
        return len(column)


def cores_of(mesh):
    row = list(mesh.devices[0, :])
    try:
        lead = row[0].coords
        return sum(1 for _ in itertools.takewhile(lambda d: d.coords == lead, row))
    except AttributeError:
        return 1


def solution(mesh):
    rows, cols = mesh.shape["rows"], mesh.shape["cols"]
    cores = cores_of(mesh)
    if cols % cores:
        cores = 1
    inner = inner_of(mesh)
    if rows % inner:
        inner = rows
    shape = (rows // inner, inner, cols // cores, cores)
    grid = Mesh(mesh.devices.reshape(shape), ROWS + COLS)
    in_specs = (P(ROWS, None), P(COLS, None), P(COLS), P(ROWS), P(COLS), P(ROWS, None))
    out_specs = (P(ROWS + COLS, None), P(COLS, None))
    body = functools.partial(local, rows, inner, cols)
    return jax.shard_map(body, mesh=grid, in_specs=in_specs, out_specs=out_specs, check_vma=False)
```

```python
import functools
import itertools
import math

import jax
import jax.numpy as jnp
from jax import lax
from jax.sharding import Mesh, PartitionSpec as P

TEMPER = 0.05


def unit_rows(matrix):
    wide = matrix.astype(jnp.float32)
    length = jnp.sqrt(jnp.sum(wide * wide, axis=1) + 1e-06)
    return ((wide / length[:, None]).astype(jnp.bfloat16), length)


def unit_back(grad, unit, length):
    wide = unit.astype(jnp.float32)
    along = jnp.sum(wide * grad, axis=1, keepdims=True)
    return (grad - wide * along) / length[:, None]


def pair_dot(left, right):
    return lax.dot_general(
        left, right, (((1,), (1,)), ((), ())), preferred_element_type=jnp.float32
    )


COLS = ("chips", "core")
ROWS = ("slab", "lane")


def across_slots(stack):
    return lax.psum(lax.psum(stack, "core"), "chips")


def exchange_sum(stack, axis, count):
    pieces = lax.all_to_all(stack.reshape(count, -1), axis, 0, 0)
    return jnp.sum(pieces, axis=0)


def exchange_gather(piece, axis, count, shape):
    copies = jnp.broadcast_to(piece.reshape(1, -1), (count, piece.size))
    return lax.all_to_all(copies, axis, 0, 0).reshape(shape)


def spread_sum(stack, axis, count):
    copies = jnp.broadcast_to(stack.reshape(1, -1), (count, stack.size))
    return jnp.sum(lax.all_to_all(copies, axis, 0, 0), axis=0).reshape(stack.shape)


def across_queries(stack, count, inner, spread=False, mixed=False):
    if mixed and stack.size % inner == 0:
        piece = spread_sum(exchange_sum(stack, "lane", inner), "slab", count // inner)
        return exchange_gather(piece, "lane", inner, stack.shape)
    if spread:
        return spread_sum(spread_sum(stack, "lane", inner), "slab", count // inner)
    if stack.size % count == 0:
        return exchange_gather(exchange_sum(stack, ROWS, count), ROWS, count, stack.shape)
    if count & (count - 1):
        return lax.psum(stack, ROWS)
    step = 1
    while step < count:
        pairs = [(i, i ^ step) for i in range(count)]
        stack = stack + lax.ppermute(stack, ROWS, pairs)
        step *= 2
    return stack


def halving_scatter(block, axis, count):
    where = lax.axis_index(axis)
    step = count // 2
    while step >= 1:
        half = block.shape[0] // 2
        bit = (where // step) % 2
        keep = lax.dynamic_slice_in_dim(block, bit * half, half, 0)
        send = lax.dynamic_slice_in_dim(block, (1 - bit) * half, half, 0)
        pairs = [(i, i ^ step) for i in range(count)]
        block = keep + lax.ppermute(send, axis, pairs)
        step //= 2
    return block


def butterfly(block, axis, count, order):
    where = lax.axis_index(axis)
    for step in order:
        half = block.shape[0] // 2
        bit = (where // step) % 2
        keep = lax.dynamic_slice_in_dim(block, bit * half, half, 0)
        send = lax.dynamic_slice_in_dim(block, (1 - bit) * half, half, 0)
        pairs = [(i, i ^ step) for i in range(count)]
        block = keep + lax.ppermute(send, axis, pairs)
    for step in reversed(order):
        bit = (where // step) % 2
        pairs = [(i, i ^ step) for i in range(count)]
        other = lax.ppermute(block, axis, pairs)
        block = jnp.where(bit == 0, jnp.concatenate([block, other]), jnp.concatenate([other, block]))
    return block


def whole_sum(block, count, inner):
    bits = [1 << k for k in range(count.bit_length() - 1)]
    if count & (count - 1) or inner >= count or block.shape[0] % (2 * count):
        return lax.psum(block, ROWS)
    low = [b for b in bits if b < inner]
    high = [b for b in bits if b >= inner]
    half = block.shape[0] // 2
    first = butterfly(block[:half], ROWS, count, low + high)
    second = butterfly(block[half:], ROWS, count, high + low)
    return jnp.concatenate([first, second])


def local(count, inner, width_cols, queries, prototypes, potential, weights, capacity, cotangent):
    qhat, qlen = unit_rows(queries)
    phat, plen = unit_rows(prototypes)
    wgt = weights.astype(jnp.float32)
    scaled = (cotangent.astype(jnp.float32) / wgt[:, None]).astype(jnp.bfloat16)
    local_rows = qhat.shape[0]
    slots = phat.shape[0]
    width = math.gcd(slots, 512)
    starts = list(range(0, slots, width))

    def kernel_tile(start):
        scores = pair_dot(qhat, phat[start : start + width])
        weight_cols = capacity[start : start + width].astype(jnp.float32)
        return weight_cols[None, :] * jnp.exp(
            (scores - potential[start : start + width][None, :]) / TEMPER
        )

    def coupling_tile(start):
        return pair_dot(scaled, phat[start : start + width])

    ztot = jnp.zeros((local_rows,), jnp.float32)
    kgsum = jnp.zeros((local_rows,), jnp.float32)
    for start in starts:
        kern = kernel_tile(start)
        ztot = ztot + jnp.sum(kern, axis=1)
        kgsum = kgsum + jnp.sum(kern * coupling_tile(start), axis=1)
    totals = across_slots(jnp.stack([ztot, kgsum]))
    share = wgt / totals[0]
    pvec = share * totals[1]
    alpha_one = pvec / wgt
    col_parts, q_parts, t_parts = ([], [], [])
    for start in starts:
        plan = share[:, None] * kernel_tile(start)
        col_parts.append(jnp.sum(plan, axis=0))
        q_parts.append(jnp.sum(plan * coupling_tile(start), axis=0))
    for start in starts:
        plan = share[:, None] * kernel_tile(start)
        t_parts.append(jnp.sum(alpha_one[:, None] * plan, axis=0))
    summed = across_queries(
        jnp.stack([jnp.concatenate(col_parts), jnp.concatenate(q_parts), jnp.concatenate(t_parts)]),
        count,
        inner,
        spread=True,
        mixed=True,
    )
    colsum, qvec, t_one = (summed[0], summed[1], summed[2])
    beta_one = (qvec - t_one) / colsum
    rowprod = jnp.zeros((local_rows,), jnp.float32)
    for start in starts:
        plan = share[:, None] * kernel_tile(start)
        rowprod = rowprod + jnp.sum(plan * beta_one[start : start + width][None, :], axis=1)
    rowprod = across_slots(rowprod[None, :])[0]
    alpha_two = (pvec - rowprod) / wgt
    t_parts = []
    for start in starts:
        plan = share[:, None] * kernel_tile(start)
        t_parts.append(jnp.sum(alpha_two[:, None] * plan, axis=0))
    t_two = across_queries(jnp.concatenate(t_parts)[None, :], count, inner, spread=True)[0]
    beta_two = (qvec - t_two) / colsum
    dqhat = jnp.zeros(qhat.shape, jnp.float32)
    dp_parts = []
    for start in starts:
        plan = share[:, None] * kernel_tile(start)
        coupling = coupling_tile(start)
        shift_cols = beta_two[start : start + width][None, :]
        dscore = (plan * (coupling - alpha_two[:, None] - shift_cols) / TEMPER).astype(jnp.bfloat16)
        planb = plan.astype(jnp.bfloat16)
        dqhat = dqhat + jnp.dot(
            dscore, phat[start : start + width], preferred_element_type=jnp.float32
        )
        part = lax.dot_general(
            dscore, qhat, (((0,), (0,)), ((), ())), preferred_element_type=jnp.float32
        )
        part = part + lax.dot_general(
            planb, scaled, (((0,), (0,)), ((), ())), preferred_element_type=jnp.float32
        )
        dp_parts.append(part)
    dphat = jnp.concatenate(dp_parts, axis=0)
    if local_rows % width_cols:
        query_part = lax.psum_scatter(dqhat, COLS, scatter_dimension=0, tiled=True)
    else:
        query_part = halving_scatter(dqhat, COLS, width_cols)
    piece = query_part.shape[0]
    begin = lax.axis_index(COLS) * piece
    grad_queries = unit_back(
        query_part,
        lax.dynamic_slice_in_dim(qhat, begin, piece, 0),
        lax.dynamic_slice_in_dim(qlen, begin, piece, 0),
    )
    if slots % count:
        grad_protos = unit_back(whole_sum(dphat, count, inner), phat, plen)
    else:
        own = slots // count
        first = lax.axis_index(ROWS) * own
        summed = exchange_sum(dphat, ROWS, count).reshape(own, dphat.shape[1])
        piece = unit_back(
            summed,
            lax.dynamic_slice_in_dim(phat, first, own, 0),
            lax.dynamic_slice_in_dim(plen, first, own, 0),
        )
        grad_protos = exchange_gather(piece, ROWS, count, dphat.shape)
    return (grad_queries, grad_protos)


def inner_of(mesh):
    column = list(mesh.devices[:, 0])
    try:
        lead = column[0].coords[1]
        return sum(1 for _ in itertools.takewhile(lambda d: d.coords[1] == lead, column))
    except (AttributeError, IndexError):
        return len(column)


def cores_of(mesh):
    row = list(mesh.devices[0, :])
    try:
        lead = row[0].coords
        return sum(1 for _ in itertools.takewhile(lambda d: d.coords == lead, row))
    except AttributeError:
        return 1


def solution(mesh):
    rows, cols = mesh.shape["rows"], mesh.shape["cols"]
    cores = cores_of(mesh)
    if cols % cores:
        cores = 1
    inner = inner_of(mesh)
    if rows % inner:
        inner = rows
    shape = (rows // inner, inner, cols // cores, cores)
    grid = Mesh(mesh.devices.reshape(shape), ROWS + COLS)
    in_specs = (P(ROWS, None), P(COLS, None), P(COLS), P(ROWS), P(COLS), P(ROWS, None))
    out_specs = (P(ROWS + COLS, None), P(COLS, None))
    body = functools.partial(local, rows, inner, cols)
    return jax.shard_map(body, mesh=grid, in_specs=in_specs, out_specs=out_specs, check_vma=False)
```

```python
import functools
import itertools
import math

import jax
import jax.numpy as jnp
from jax import lax
from jax.sharding import Mesh, PartitionSpec as P

TEMPER = 0.05


def unit_rows(matrix):
    wide = matrix.astype(jnp.float32)
    length = jnp.sqrt(jnp.sum(wide * wide, axis=1) + 1e-06)
    return ((wide / length[:, None]).astype(jnp.bfloat16), length)


def unit_back(grad, unit, length):
    wide = unit.astype(jnp.float32)
    along = jnp.sum(wide * grad, axis=1, keepdims=True)
    return (grad - wide * along) / length[:, None]


def pair_dot(left, right):
    return lax.dot_general(
        left, right, (((1,), (1,)), ((), ())), preferred_element_type=jnp.float32
    )


COLS = ("chips", "core")
ROWS = ("slab", "lane")


def across_slots(stack, chips):
    return spread_sum(lax.psum(stack, "core"), "chips", chips)


def exchange_sum(stack, axis, count):
    pieces = lax.all_to_all(stack.reshape(count, -1), axis, 0, 0)
    return jnp.sum(pieces, axis=0)


def exchange_gather(piece, axis, count, shape):
    copies = jnp.broadcast_to(piece.reshape(1, -1), (count, piece.size))
    return lax.all_to_all(copies, axis, 0, 0).reshape(shape)


def spread_sum(stack, axis, count):
    copies = jnp.broadcast_to(stack.reshape(1, -1), (count, stack.size))
    return jnp.sum(lax.all_to_all(copies, axis, 0, 0), axis=0).reshape(stack.shape)


def across_queries(stack, count, inner, spread=False):
    if spread:
        return spread_sum(spread_sum(stack, "lane", inner), "slab", count // inner)
    if stack.size % count == 0:
        return exchange_gather(exchange_sum(stack, ROWS, count), ROWS, count, stack.shape)
    if count & (count - 1):
        return lax.psum(stack, ROWS)
    step = 1
    while step < count:
        pairs = [(i, i ^ step) for i in range(count)]
        stack = stack + lax.ppermute(stack, ROWS, pairs)
        step *= 2
    return stack


def halving_scatter(block, axis, count):
    where = lax.axis_index(axis)
    step = count // 2
    while step >= 1:
        half = block.shape[0] // 2
        bit = (where // step) % 2
        keep = lax.dynamic_slice_in_dim(block, bit * half, half, 0)
        send = lax.dynamic_slice_in_dim(block, (1 - bit) * half, half, 0)
        pairs = [(i, i ^ step) for i in range(count)]
        block = keep + lax.ppermute(send, axis, pairs)
        step //= 2
    return block


def butterfly(block, axis, count, order):
    where = lax.axis_index(axis)
    for step in order:
        half = block.shape[0] // 2
        bit = (where // step) % 2
        keep = lax.dynamic_slice_in_dim(block, bit * half, half, 0)
        send = lax.dynamic_slice_in_dim(block, (1 - bit) * half, half, 0)
        pairs = [(i, i ^ step) for i in range(count)]
        block = keep + lax.ppermute(send, axis, pairs)
    for step in reversed(order):
        bit = (where // step) % 2
        pairs = [(i, i ^ step) for i in range(count)]
        other = lax.ppermute(block, axis, pairs)
        block = jnp.where(bit == 0, jnp.concatenate([block, other]), jnp.concatenate([other, block]))
    return block


def whole_sum(block, count, inner):
    bits = [1 << k for k in range(count.bit_length() - 1)]
    if count & (count - 1) or inner >= count or block.shape[0] % (2 * count):
        return lax.psum(block, ROWS)
    low = [b for b in bits if b < inner]
    high = [b for b in bits if b >= inner]
    half = block.shape[0] // 2
    first = butterfly(block[:half], ROWS, count, low + high)
    second = butterfly(block[half:], ROWS, count, high + low)
    return jnp.concatenate([first, second])


def local(count, inner, width_cols, chips, queries, prototypes, potential, weights, capacity, cotangent):
    qhat, qlen = unit_rows(queries)
    phat, plen = unit_rows(prototypes)
    wgt = weights.astype(jnp.float32)
    scaled = (cotangent.astype(jnp.float32) / wgt[:, None]).astype(jnp.bfloat16)
    local_rows = qhat.shape[0]
    slots = phat.shape[0]
    width = math.gcd(slots, 512)
    starts = list(range(0, slots, width))

    def kernel_tile(start):
        scores = pair_dot(qhat, phat[start : start + width])
        weight_cols = capacity[start : start + width].astype(jnp.float32)
        return weight_cols[None, :] * jnp.exp(
            (scores - potential[start : start + width][None, :]) / TEMPER
        )

    def coupling_tile(start):
        return pair_dot(scaled, phat[start : start + width])

    ztot = jnp.zeros((local_rows,), jnp.float32)
    kgsum = jnp.zeros((local_rows,), jnp.float32)
    for start in starts:
        kern = kernel_tile(start)
        ztot = ztot + jnp.sum(kern, axis=1)
        kgsum = kgsum + jnp.sum(kern * coupling_tile(start), axis=1)
    totals = across_slots(jnp.stack([ztot, kgsum]), chips)
    share = wgt / totals[0]
    pvec = share * totals[1]
    alpha_one = pvec / wgt
    col_parts, q_parts, t_parts = ([], [], [])
    for start in starts:
        plan = share[:, None] * kernel_tile(start)
        col_parts.append(jnp.sum(plan, axis=0))
        q_parts.append(jnp.sum(plan * coupling_tile(start), axis=0))
    for start in starts:
        plan = share[:, None] * kernel_tile(start)
        t_parts.append(jnp.sum(alpha_one[:, None] * plan, axis=0))
    summed = across_queries(
        jnp.stack([jnp.concatenate(col_parts), jnp.concatenate(q_parts), jnp.concatenate(t_parts)]),
        count,
        inner,
        spread=True,
    )
    colsum, qvec, t_one = (summed[0], summed[1], summed[2])
    beta_one = (qvec - t_one) / colsum
    rowprod = jnp.zeros((local_rows,), jnp.float32)
    for start in starts:
        plan = share[:, None] * kernel_tile(start)
        rowprod = rowprod + jnp.sum(plan * beta_one[start : start + width][None, :], axis=1)
    rowprod = across_slots(rowprod[None, :], chips)[0]
    alpha_two = (pvec - rowprod) / wgt
    t_parts = []
    for start in starts:
        plan = share[:, None] * kernel_tile(start)
        t_parts.append(jnp.sum(alpha_two[:, None] * plan, axis=0))
    t_two = across_queries(jnp.concatenate(t_parts)[None, :], count, inner, spread=True)[0]
    beta_two = (qvec - t_two) / colsum
    dqhat = jnp.zeros(qhat.shape, jnp.float32)
    dp_parts = []
    for start in starts:
        plan = share[:, None] * kernel_tile(start)
        coupling = coupling_tile(start)
        shift_cols = beta_two[start : start + width][None, :]
        dscore = (plan * (coupling - alpha_two[:, None] - shift_cols) / TEMPER).astype(jnp.bfloat16)
        planb = plan.astype(jnp.bfloat16)
        dqhat = dqhat + jnp.dot(
            dscore, phat[start : start + width], preferred_element_type=jnp.float32
        )
        part = lax.dot_general(
            dscore, qhat, (((0,), (0,)), ((), ())), preferred_element_type=jnp.float32
        )
        part = part + lax.dot_general(
            planb, scaled, (((0,), (0,)), ((), ())), preferred_element_type=jnp.float32
        )
        dp_parts.append(part)
    dphat = jnp.concatenate(dp_parts, axis=0)
    if local_rows % width_cols:
        query_part = lax.psum_scatter(dqhat, COLS, scatter_dimension=0, tiled=True)
    else:
        query_part = halving_scatter(dqhat, COLS, width_cols)
    piece = query_part.shape[0]
    begin = lax.axis_index(COLS) * piece
    grad_queries = unit_back(
        query_part,
        lax.dynamic_slice_in_dim(qhat, begin, piece, 0),
        lax.dynamic_slice_in_dim(qlen, begin, piece, 0),
    )
    if slots % count:
        grad_protos = unit_back(whole_sum(dphat, count, inner), phat, plen)
    else:
        own = slots // count
        first = lax.axis_index(ROWS) * own
        summed = exchange_sum(dphat, ROWS, count).reshape(own, dphat.shape[1])
        piece = unit_back(
            summed,
            lax.dynamic_slice_in_dim(phat, first, own, 0),
            lax.dynamic_slice_in_dim(plen, first, own, 0),
        )
        grad_protos = exchange_gather(piece, ROWS, count, dphat.shape)
    return (grad_queries, grad_protos)


def inner_of(mesh):
    column = list(mesh.devices[:, 0])
    try:
        lead = column[0].coords[1]
        return sum(1 for _ in itertools.takewhile(lambda d: d.coords[1] == lead, column))
    except (AttributeError, IndexError):
        return len(column)


def cores_of(mesh):
    row = list(mesh.devices[0, :])
    try:
        lead = row[0].coords
        return sum(1 for _ in itertools.takewhile(lambda d: d.coords == lead, row))
    except AttributeError:
        return 1


def solution(mesh):
    rows, cols = mesh.shape["rows"], mesh.shape["cols"]
    cores = cores_of(mesh)
    if cols % cores:
        cores = 1
    inner = inner_of(mesh)
    if rows % inner:
        inner = rows
    shape = (rows // inner, inner, cols // cores, cores)
    grid = Mesh(mesh.devices.reshape(shape), ROWS + COLS)
    in_specs = (P(ROWS, None), P(COLS, None), P(COLS), P(ROWS), P(COLS), P(ROWS, None))
    out_specs = (P(ROWS + COLS, None), P(COLS, None))
    body = functools.partial(local, rows, inner, cols, cols // cores)
    return jax.shard_map(body, mesh=grid, in_specs=in_specs, out_specs=out_specs, check_vma=False)
```

```python
import functools
import itertools
import math

import jax
import jax.numpy as jnp
from jax import lax
from jax.sharding import Mesh, PartitionSpec as P

TEMPER = 0.05


def unit_rows(matrix):
    wide = matrix.astype(jnp.float32)
    length = jnp.sqrt(jnp.sum(wide * wide, axis=1) + 1e-06)
    return ((wide / length[:, None]).astype(jnp.bfloat16), length)


def unit_back(grad, unit, length):
    wide = unit.astype(jnp.float32)
    along = jnp.sum(wide * grad, axis=1, keepdims=True)
    return (grad - wide * along) / length[:, None]


def pair_dot(left, right):
    return lax.dot_general(
        left, right, (((1,), (1,)), ((), ())), preferred_element_type=jnp.float32
    )


COLS = ("chips", "core")
ROWS = ("slab", "lane")


def across_slots(stack, chips):
    return spread_sum(lax.psum(stack, "core"), "chips", chips)


def exchange_sum(stack, axis, count):
    pieces = lax.all_to_all(stack.reshape(count, -1), axis, 0, 0)
    return jnp.sum(pieces, axis=0)


def exchange_gather(piece, axis, count, shape):
    copies = jnp.broadcast_to(piece.reshape(1, -1), (count, piece.size))
    return lax.all_to_all(copies, axis, 0, 0).reshape(shape)


def spread_sum(stack, axis, count):
    copies = jnp.broadcast_to(stack.reshape(1, -1), (count, stack.size))
    return jnp.sum(lax.all_to_all(copies, axis, 0, 0), axis=0).reshape(stack.shape)


def across_queries(stack, count, inner, spread=False):
    if spread:
        return spread_sum(spread_sum(stack, "lane", inner), "slab", count // inner)
    if stack.size % count == 0:
        return exchange_gather(exchange_sum(stack, ROWS, count), ROWS, count, stack.shape)
    if count & (count - 1):
        return lax.psum(stack, ROWS)
    step = 1
    while step < count:
        pairs = [(i, i ^ step) for i in range(count)]
        stack = stack + lax.ppermute(stack, ROWS, pairs)
        step *= 2
    return stack


def halving_scatter(block, axis, count):
    where = lax.axis_index(axis)
    step = count // 2
    while step >= 1:
        half = block.shape[0] // 2
        bit = (where // step) % 2
        keep = lax.dynamic_slice_in_dim(block, bit * half, half, 0)
        send = lax.dynamic_slice_in_dim(block, (1 - bit) * half, half, 0)
        pairs = [(i, i ^ step) for i in range(count)]
        block = keep + lax.ppermute(send, axis, pairs)
        step //= 2
    return block


def butterfly(block, axis, count, order):
    where = lax.axis_index(axis)
    for step in order:
        half = block.shape[0] // 2
        bit = (where // step) % 2
        keep = lax.dynamic_slice_in_dim(block, bit * half, half, 0)
        send = lax.dynamic_slice_in_dim(block, (1 - bit) * half, half, 0)
        pairs = [(i, i ^ step) for i in range(count)]
        block = keep + lax.ppermute(send, axis, pairs)
    for step in reversed(order):
        bit = (where // step) % 2
        pairs = [(i, i ^ step) for i in range(count)]
        other = lax.ppermute(block, axis, pairs)
        block = jnp.where(bit == 0, jnp.concatenate([block, other]), jnp.concatenate([other, block]))
    return block


def whole_sum(block, count, inner):
    bits = [1 << k for k in range(count.bit_length() - 1)]
    if count & (count - 1) or inner >= count or block.shape[0] % (2 * count):
        return lax.psum(block, ROWS)
    low = [b for b in bits if b < inner]
    high = [b for b in bits if b >= inner]
    half = block.shape[0] // 2
    first = butterfly(block[:half], ROWS, count, low + high)
    second = butterfly(block[half:], ROWS, count, high + low)
    return jnp.concatenate([first, second])


def local(count, inner, width_cols, chips, queries, prototypes, potential, weights, capacity, cotangent):
    qhat, qlen = unit_rows(queries)
    phat, plen = unit_rows(prototypes)
    wgt = weights.astype(jnp.float32)
    scaled = (cotangent.astype(jnp.float32) / wgt[:, None]).astype(jnp.bfloat16)
    local_rows = qhat.shape[0]
    slots = phat.shape[0]
    width = math.gcd(slots, 512)
    starts = list(range(0, slots, width))

    def kernel_tile(start):
        scores = pair_dot(qhat, phat[start : start + width])
        weight_cols = capacity[start : start + width].astype(jnp.float32)
        return weight_cols[None, :] * jnp.exp(
            (scores - potential[start : start + width][None, :]) / TEMPER
        )

    def coupling_tile(start):
        return pair_dot(scaled, phat[start : start + width])

    ztot = jnp.zeros((local_rows,), jnp.float32)
    kgsum = jnp.zeros((local_rows,), jnp.float32)
    for start in starts:
        kern = kernel_tile(start)
        ztot = ztot + jnp.sum(kern, axis=1)
        kgsum = kgsum + jnp.sum(kern * coupling_tile(start), axis=1)
    totals = across_slots(jnp.stack([ztot, kgsum]), chips)
    share = wgt / totals[0]
    pvec = share * totals[1]
    alpha_one = pvec / wgt
    col_parts, q_parts, t_parts = ([], [], [])
    for start in starts:
        plan = share[:, None] * kernel_tile(start)
        col_parts.append(jnp.sum(plan, axis=0))
        q_parts.append(jnp.sum(plan * (coupling_tile(start) - alpha_one[:, None]), axis=0))
    summed = across_queries(
        jnp.stack([jnp.concatenate(col_parts), jnp.concatenate(q_parts)]),
        count,
        inner,
        spread=True,
    )
    colsum, first_gap = (summed[0], summed[1])
    beta_one = first_gap / colsum
    rowprod = jnp.zeros((local_rows,), jnp.float32)
    for start in starts:
        plan = share[:, None] * kernel_tile(start)
        rowprod = rowprod + jnp.sum(plan * beta_one[start : start + width][None, :], axis=1)
    rowprod = across_slots(rowprod[None, :], chips)[0]
    alpha_two = (pvec - rowprod) / wgt
    t_parts = []
    for start in starts:
        plan = share[:, None] * kernel_tile(start)
        t_parts.append(jnp.sum((alpha_one - alpha_two)[:, None] * plan, axis=0))
    t_two = across_queries(jnp.concatenate(t_parts)[None, :], count, inner, spread=True)[0]
    beta_two = (first_gap + t_two) / colsum
    dqhat = jnp.zeros(qhat.shape, jnp.float32)
    dp_parts = []
    for start in starts:
        plan = share[:, None] * kernel_tile(start)
        coupling = coupling_tile(start)
        shift_cols = beta_two[start : start + width][None, :]
        dscore = (plan * (coupling - alpha_two[:, None] - shift_cols) / TEMPER).astype(jnp.bfloat16)
        planb = plan.astype(jnp.bfloat16)
        dqhat = dqhat + jnp.dot(
            dscore, phat[start : start + width], preferred_element_type=jnp.float32
        )
        part = lax.dot_general(
            dscore, qhat, (((0,), (0,)), ((), ())), preferred_element_type=jnp.float32
        )
        part = part + lax.dot_general(
            planb, scaled, (((0,), (0,)), ((), ())), preferred_element_type=jnp.float32
        )
        dp_parts.append(part)
    dphat = jnp.concatenate(dp_parts, axis=0)
    if local_rows % width_cols:
        query_part = lax.psum_scatter(dqhat, COLS, scatter_dimension=0, tiled=True)
    else:
        query_part = halving_scatter(dqhat, COLS, width_cols)
    piece = query_part.shape[0]
    begin = lax.axis_index(COLS) * piece
    grad_queries = unit_back(
        query_part,
        lax.dynamic_slice_in_dim(qhat, begin, piece, 0),
        lax.dynamic_slice_in_dim(qlen, begin, piece, 0),
    )
    if slots % count:
        grad_protos = unit_back(whole_sum(dphat, count, inner), phat, plen)
    else:
        own = slots // count
        first = lax.axis_index(ROWS) * own
        summed = exchange_sum(dphat, ROWS, count).reshape(own, dphat.shape[1])
        piece = unit_back(
            summed,
            lax.dynamic_slice_in_dim(phat, first, own, 0),
            lax.dynamic_slice_in_dim(plen, first, own, 0),
        )
        grad_protos = exchange_gather(piece, ROWS, count, dphat.shape)
    return (grad_queries, grad_protos)


def inner_of(mesh):
    column = list(mesh.devices[:, 0])
    try:
        lead = column[0].coords[1]
        return sum(1 for _ in itertools.takewhile(lambda d: d.coords[1] == lead, column))
    except (AttributeError, IndexError):
        return len(column)


def cores_of(mesh):
    row = list(mesh.devices[0, :])
    try:
        lead = row[0].coords
        return sum(1 for _ in itertools.takewhile(lambda d: d.coords == lead, row))
    except AttributeError:
        return 1


def solution(mesh):
    rows, cols = mesh.shape["rows"], mesh.shape["cols"]
    cores = cores_of(mesh)
    if cols % cores:
        cores = 1
    inner = inner_of(mesh)
    if rows % inner:
        inner = rows
    shape = (rows // inner, inner, cols // cores, cores)
    grid = Mesh(mesh.devices.reshape(shape), ROWS + COLS)
    in_specs = (P(ROWS, None), P(COLS, None), P(COLS), P(ROWS), P(COLS), P(ROWS, None))
    out_specs = (P(ROWS + COLS, None), P(COLS, None))
    body = functools.partial(local, rows, inner, cols, cols // cores)
    return jax.shard_map(body, mesh=grid, in_specs=in_specs, out_specs=out_specs, check_vma=False)
```

```python
import functools
import itertools
import math

import jax
import jax.numpy as jnp
from jax import lax
from jax.sharding import Mesh, PartitionSpec as P

TEMPER = 0.05


def unit_rows(matrix):
    wide = matrix.astype(jnp.float32)
    length = jnp.sqrt(jnp.sum(wide * wide, axis=1) + 1e-06)
    return ((wide / length[:, None]).astype(jnp.bfloat16), length)


def unit_back(grad, unit, length):
    wide = unit.astype(jnp.float32)
    along = jnp.sum(wide * grad, axis=1, keepdims=True)
    return (grad - wide * along) / length[:, None]


def pair_dot(left, right):
    return lax.dot_general(
        left, right, (((1,), (1,)), ((), ())), preferred_element_type=jnp.float32
    )


COLS = ("chips", "core")
ROWS = ("slab", "lane")


def across_slots(stack, width):
    return spread_sum(stack, COLS, width)


def exchange_sum(stack, axis, count):
    pieces = lax.all_to_all(stack.reshape(count, -1), axis, 0, 0)
    return jnp.sum(pieces, axis=0)


def exchange_gather(piece, axis, count, shape):
    copies = jnp.broadcast_to(piece.reshape(1, -1), (count, piece.size))
    return lax.all_to_all(copies, axis, 0, 0).reshape(shape)


def spread_sum(stack, axis, count):
    copies = jnp.broadcast_to(stack.reshape(1, -1), (count, stack.size))
    return jnp.sum(lax.all_to_all(copies, axis, 0, 0), axis=0).reshape(stack.shape)


def across_queries(stack, count, inner, spread=False):
    if spread:
        return spread_sum(spread_sum(stack, "lane", inner), "slab", count // inner)
    if stack.size % count == 0:
        return exchange_gather(exchange_sum(stack, ROWS, count), ROWS, count, stack.shape)
    if count & (count - 1):
        return lax.psum(stack, ROWS)
    step = 1
    while step < count:
        pairs = [(i, i ^ step) for i in range(count)]
        stack = stack + lax.ppermute(stack, ROWS, pairs)
        step *= 2
    return stack


def halving_scatter(block, axis, count):
    where = lax.axis_index(axis)
    step = count // 2
    while step >= 1:
        half = block.shape[0] // 2
        bit = (where // step) % 2
        keep = lax.dynamic_slice_in_dim(block, bit * half, half, 0)
        send = lax.dynamic_slice_in_dim(block, (1 - bit) * half, half, 0)
        pairs = [(i, i ^ step) for i in range(count)]
        block = keep + lax.ppermute(send, axis, pairs)
        step //= 2
    return block


def butterfly(block, axis, count, order):
    where = lax.axis_index(axis)
    for step in order:
        half = block.shape[0] // 2
        bit = (where // step) % 2
        keep = lax.dynamic_slice_in_dim(block, bit * half, half, 0)
        send = lax.dynamic_slice_in_dim(block, (1 - bit) * half, half, 0)
        pairs = [(i, i ^ step) for i in range(count)]
        block = keep + lax.ppermute(send, axis, pairs)
    for step in reversed(order):
        bit = (where // step) % 2
        pairs = [(i, i ^ step) for i in range(count)]
        other = lax.ppermute(block, axis, pairs)
        block = jnp.where(bit == 0, jnp.concatenate([block, other]), jnp.concatenate([other, block]))
    return block


def whole_sum(block, count, inner):
    bits = [1 << k for k in range(count.bit_length() - 1)]
    if count & (count - 1) or inner >= count or block.shape[0] % (2 * count):
        return lax.psum(block, ROWS)
    low = [b for b in bits if b < inner]
    high = [b for b in bits if b >= inner]
    half = block.shape[0] // 2
    first = butterfly(block[:half], ROWS, count, low + high)
    second = butterfly(block[half:], ROWS, count, high + low)
    return jnp.concatenate([first, second])


def local(count, inner, width_cols, chips, queries, prototypes, potential, weights, capacity, cotangent):
    qhat, qlen = unit_rows(queries)
    phat, plen = unit_rows(prototypes)
    wgt = weights.astype(jnp.float32)
    scaled = (cotangent.astype(jnp.float32) / wgt[:, None]).astype(jnp.bfloat16)
    local_rows = qhat.shape[0]
    slots = phat.shape[0]
    width = math.gcd(slots, 512)
    starts = list(range(0, slots, width))

    def kernel_tile(start):
        scores = pair_dot(qhat, phat[start : start + width])
        weight_cols = capacity[start : start + width].astype(jnp.float32)
        return weight_cols[None, :] * jnp.exp(
            (scores - potential[start : start + width][None, :]) / TEMPER
        )

    def coupling_tile(start):
        return pair_dot(scaled, phat[start : start + width])

    ztot = jnp.zeros((local_rows,), jnp.float32)
    kgsum = jnp.zeros((local_rows,), jnp.float32)
    for start in starts:
        kern = kernel_tile(start)
        ztot = ztot + jnp.sum(kern, axis=1)
        kgsum = kgsum + jnp.sum(kern * coupling_tile(start), axis=1)
    totals = across_slots(jnp.stack([ztot, kgsum]), chips)
    share = wgt / totals[0]
    pvec = share * totals[1]
    alpha_one = pvec / wgt
    col_parts, q_parts, t_parts = ([], [], [])
    for start in starts:
        plan = share[:, None] * kernel_tile(start)
        col_parts.append(jnp.sum(plan, axis=0))
        q_parts.append(jnp.sum(plan * coupling_tile(start), axis=0))
    for start in starts:
        plan = share[:, None] * kernel_tile(start)
        t_parts.append(jnp.sum(alpha_one[:, None] * plan, axis=0))
    summed = across_queries(
        jnp.stack([jnp.concatenate(col_parts), jnp.concatenate(q_parts), jnp.concatenate(t_parts)]),
        count,
        inner,
        spread=True,
    )
    colsum, qvec, t_one = (summed[0], summed[1], summed[2])
    beta_one = (qvec - t_one) / colsum
    rowprod = jnp.zeros((local_rows,), jnp.float32)
    for start in starts:
        plan = share[:, None] * kernel_tile(start)
        rowprod = rowprod + jnp.sum(plan * beta_one[start : start + width][None, :], axis=1)
    rowprod = across_slots(rowprod[None, :], chips)[0]
    alpha_two = (pvec - rowprod) / wgt
    t_parts = []
    for start in starts:
        plan = share[:, None] * kernel_tile(start)
        t_parts.append(jnp.sum(alpha_two[:, None] * plan, axis=0))
    t_two = across_queries(jnp.concatenate(t_parts)[None, :], count, inner, spread=True)[0]
    beta_two = (qvec - t_two) / colsum
    dqhat = jnp.zeros(qhat.shape, jnp.float32)
    dp_parts = []
    for start in starts:
        plan = share[:, None] * kernel_tile(start)
        coupling = coupling_tile(start)
        shift_cols = beta_two[start : start + width][None, :]
        dscore = (plan * (coupling - alpha_two[:, None] - shift_cols) / TEMPER).astype(jnp.bfloat16)
        planb = plan.astype(jnp.bfloat16)
        dqhat = dqhat + jnp.dot(
            dscore, phat[start : start + width], preferred_element_type=jnp.float32
        )
        part = lax.dot_general(
            dscore, qhat, (((0,), (0,)), ((), ())), preferred_element_type=jnp.float32
        )
        part = part + lax.dot_general(
            planb, scaled, (((0,), (0,)), ((), ())), preferred_element_type=jnp.float32
        )
        dp_parts.append(part)
    dphat = jnp.concatenate(dp_parts, axis=0)
    if local_rows % width_cols:
        query_part = lax.psum_scatter(dqhat, COLS, scatter_dimension=0, tiled=True)
    else:
        query_part = halving_scatter(dqhat, COLS, width_cols)
    piece = query_part.shape[0]
    begin = lax.axis_index(COLS) * piece
    grad_queries = unit_back(
        query_part,
        lax.dynamic_slice_in_dim(qhat, begin, piece, 0),
        lax.dynamic_slice_in_dim(qlen, begin, piece, 0),
    )
    if slots % count:
        grad_protos = unit_back(whole_sum(dphat, count, inner), phat, plen)
    else:
        own = slots // count
        first = lax.axis_index(ROWS) * own
        summed = exchange_sum(dphat, ROWS, count).reshape(own, dphat.shape[1])
        piece = unit_back(
            summed,
            lax.dynamic_slice_in_dim(phat, first, own, 0),
            lax.dynamic_slice_in_dim(plen, first, own, 0),
        )
        grad_protos = exchange_gather(piece, ROWS, count, dphat.shape)
    return (grad_queries, grad_protos)


def inner_of(mesh):
    column = list(mesh.devices[:, 0])
    try:
        lead = column[0].coords[1]
        return sum(1 for _ in itertools.takewhile(lambda d: d.coords[1] == lead, column))
    except (AttributeError, IndexError):
        return len(column)


def cores_of(mesh):
    row = list(mesh.devices[0, :])
    try:
        lead = row[0].coords
        return sum(1 for _ in itertools.takewhile(lambda d: d.coords == lead, row))
    except AttributeError:
        return 1


def solution(mesh):
    rows, cols = mesh.shape["rows"], mesh.shape["cols"]
    cores = cores_of(mesh)
    if cols % cores:
        cores = 1
    inner = inner_of(mesh)
    if rows % inner:
        inner = rows
    shape = (rows // inner, inner, cols // cores, cores)
    grid = Mesh(mesh.devices.reshape(shape), ROWS + COLS)
    in_specs = (P(ROWS, None), P(COLS, None), P(COLS), P(ROWS), P(COLS), P(ROWS, None))
    out_specs = (P(ROWS + COLS, None), P(COLS, None))
    body = functools.partial(local, rows, inner, cols, cols)
    return jax.shard_map(body, mesh=grid, in_specs=in_specs, out_specs=out_specs, check_vma=False)
```
